256 devices in a mesh: tm: 2 (over core), tile: 128 (over x, z, y).
Axes of the slice: x: 4, y: 4, z: 8, core: 2. Of those that a mesh axis runs over, the one named last changes fastest.
Arguments:
- features: bfloat16 [4, 128, 128, 384], P('tm', 'tile'), may hold values from -48 to 48
- query_weight: bfloat16 [384, 384], replicated, may hold values from -1 to 1
- key_weight: bfloat16 [384, 384], replicated, may hold values from -12 to 12
- value_weight: bfloat16 [384, 384], replicated, may hold values from -0.3125 to 0.3125
- out_weight: bfloat16 [384, 384], replicated, may hold values from -1.25 to 1.25
- conv_weight: bfloat16 [3, 3, 3, 384, 384], replicated, may hold values from -0.0625 to 0.0625
Outputs:
- decoded: bfloat16 [4, 128, 128, 384], P('tm', 'tile')
The draws below stay inside these ranges and needn't reach their ends.
All inputs are finite; a program needn't handle non-finite values.
Results may differ from the reference program's by a relative error of at most 0.019.
Values may be sent and summed in bfloat16 or wider, within the bound.
No kernel may reach another device: no remote copies, remote signals or barrier semaphores. Data moves between devices by JAX's collectives and lax.ppermute only.
A program may use at most 128 MiB of HBM per device.

```python
import math
import jax
import jax.numpy as jnp
from jax import lax

D = 384
COLS = 128
FRAMES = 4
ROWS = 128


def query_base(key):
    return jnp.clip(jax.random.normal(jax.random.fold_in(key, 31), (D, D), jnp.float32), -4.0, 4.0)


def draw_features(key, part):
    values = jnp.clip(jax.random.normal(jax.random.fold_in(key, 45), (FRAMES, ROWS, COLS, D), jnp.float32), -6.0, 6.0)
    return values.astype(jnp.bfloat16)


def draw_query_weight(key, part):
    return (query_base(key) / math.sqrt(D)).astype(jnp.bfloat16)


def draw_key_weight(key, part):
    noise = jnp.clip(jax.random.normal(jax.random.fold_in(key, 32), (D, D), jnp.float32), -4.0, 4.0)
    values = 2.0 * noise / math.sqrt(D)
    return values.astype(jnp.bfloat16)


def normal_values(rng, dims, scale, most, held_as=jnp.bfloat16):
    return jnp.clip(scale * jax.random.normal(rng, dims, jnp.float32), -most, most).astype(held_as)


def setup_inputs(seed: int = 0) -> dict:
    keys = jax.random.split(jax.random.key(seed), 7)
    features = draw_features(jax.random.fold_in(keys[6], 71), 0)
    query_weight = draw_query_weight(jax.random.fold_in(keys[6], 71), 0)
    key_weight = draw_key_weight(jax.random.fold_in(keys[6], 71), 0)
    value_weight = normal_values(keys[3], (D, D), D ** -0.5, 0.3125)
    out_weight = normal_values(keys[4], (D, D), (D // 16) ** -0.5, 1.25)
    conv_weight = normal_values(keys[5], (3, 3, 3, D, D), (27 * D) ** -0.5, 0.0625)
    return {"features": features, "query_weight": query_weight, "key_weight": key_weight, "value_weight": value_weight, "out_weight": out_weight, "conv_weight": conv_weight}


def rms_rows(values):
    return values * lax.rsqrt(lax.optimization_barrier(jnp.mean(values * values, axis=-1, keepdims=True)) + 1e-06)

def frame_attention(frame_tokens, query_weight, key_weight, value_weight):
    query = jnp.dot(frame_tokens, query_weight, preferred_element_type=jnp.float32).astype(jnp.bfloat16)
    key_rows = jnp.dot(frame_tokens, key_weight, preferred_element_type=jnp.float32).astype(jnp.bfloat16)
    value_rows = jnp.dot(frame_tokens, value_weight, preferred_element_type=jnp.float32).astype(jnp.bfloat16)
    scale = 1.0 / math.sqrt(frame_tokens.shape[1])
    scores = jnp.dot(query, key_rows.T, preferred_element_type=jnp.float32) * scale
    highest = lax.optimization_barrier(jnp.max(scores, axis=-1, keepdims=True))
    expo = jnp.exp(scores - highest)
    total = lax.optimization_barrier(jnp.sum(expo, axis=-1, keepdims=True))
    probs = expo.astype(jnp.bfloat16)
    summed = jnp.dot(probs, value_rows, preferred_element_type=jnp.float32)
    return (summed / total).astype(jnp.bfloat16)

def reference(features, query_weight, key_weight, value_weight, out_weight, conv_weight):
    frames, rows, cols, width = features.shape
    widened = features.astype(jnp.float32)
    normed = rms_rows(widened).astype(jnp.bfloat16)
    attended = lax.map(lambda tokens: frame_attention(tokens, query_weight, key_weight, value_weight), normed.reshape(frames, rows * cols, width))
    projected = jnp.dot(attended.reshape(-1, width), out_weight, preferred_element_type=jnp.float32)
    mixed = (widened + projected.reshape(features.shape)).astype(jnp.bfloat16)
    mixed_wide = mixed.astype(jnp.float32)
    activated = jax.nn.silu(rms_rows(mixed_wide)).astype(jnp.bfloat16)
    padded = jnp.pad(activated, ((2, 0), (1, 1), (1, 1), (0, 0)))
    conv = jnp.zeros((frames * rows * cols, width), jnp.float32)
    for tap_time in range(3):
        for tap_row in range(3):
            for tap_col in range(3):
                window = padded[tap_time:tap_time + frames, tap_row:tap_row + rows, tap_col:tap_col + cols]
                conv = conv + jnp.dot(window.reshape(-1, width), conv_weight[tap_time, tap_row, tap_col], preferred_element_type=jnp.float32)
    return (mixed_wide + conv.reshape(features.shape)).astype(jnp.bfloat16)
```

```python
import math

import jax
import jax.numpy as jnp
from jax import lax
from jax.sharding import Mesh
from jax.sharding import PartitionSpec as P

ROW_AXES = ("x", "z", "y")


def rms_rows(values):
    return values * lax.rsqrt(jnp.mean(values * values, axis=-1, keepdims=True) + 1e-06)


def project(flat_rows, weight):
    return jnp.dot(flat_rows, weight, preferred_element_type=jnp.float32).astype(jnp.bfloat16)


def row_shift(block, forward):
    count = 1
    for name in ROW_AXES:
        count *= lax.axis_size(name)
    if forward:
        route = [(i, i + 1) for i in range(count - 1)]
    else:
        route = [(i + 1, i) for i in range(count - 1)]
    return lax.ppermute(block, ROW_AXES, route)


def per_device(features, query_weight, key_weight, value_weight, out_weight, conv_weight):
    frames, rows, cols, width = features.shape
    count = rows * cols
    widened = features.astype(jnp.float32)
    normed = rms_rows(widened).astype(jnp.bfloat16)
    flat = normed.reshape(frames * count, width)
    scale = 1.0 / math.sqrt(width)

    query = project(flat, query_weight).reshape(frames, count, width)
    query_all = lax.all_gather(query, "z", axis=1, tiled=True)
    normed_all = lax.all_gather(normed.reshape(frames, count, width), ("x", "y"), axis=1, tiled=True)
    keys_in = normed_all.reshape(-1, width)
    key_rows = project(keys_in, key_weight).reshape(frames, -1, width)
    value_rows = project(keys_in, value_weight).reshape(frames, -1, width)

    scores = jnp.einsum("fqd,fkd->fqk", query_all, key_rows, preferred_element_type=jnp.float32) * scale
    highest = lax.pmax(jnp.max(scores, axis=-1), "z")
    expo = jnp.exp(scores - highest[..., None])
    total = jnp.sum(expo, axis=-1)
    probs = expo.astype(jnp.bfloat16)
    summed = jnp.einsum("fqk,fkd->fqd", probs, value_rows, preferred_element_type=jnp.float32)
    summed = lax.psum_scatter(summed.astype(jnp.bfloat16), "z", scatter_dimension=1, tiled=True)
    total = lax.psum_scatter(total, "z", scatter_dimension=1, tiled=True)
    attended = (summed.astype(jnp.float32) / total[:, :, None]).astype(jnp.bfloat16)

    projected = jnp.dot(attended.reshape(-1, width), out_weight, preferred_element_type=jnp.float32)
    mixed = (widened + projected.reshape(features.shape)).astype(jnp.bfloat16)
    mixed_wide = mixed.astype(jnp.float32)
    activated = jax.nn.silu(rms_rows(mixed_wide)).astype(jnp.bfloat16)

    earlier = lax.ppermute(activated, "tm", [(0, 1)])
    stacked = jnp.concatenate([earlier, activated], axis=0)
    above = row_shift(stacked, True)
    below = row_shift(stacked, False)
    padded = jnp.concatenate([above, stacked, below], axis=1)
    padded = jnp.pad(padded, ((0, 0), (0, 0), (1, 1), (0, 0)))
    patches = []
    for tap_time in range(3):
        for tap_row in range(3):
            for tap_col in range(3):
                patches.append(
                    padded[
                        tap_time : tap_time + frames,
                        tap_row : tap_row + rows,
                        tap_col : tap_col + cols,
                    ]
                )
    columns = jnp.concatenate(patches, axis=-1).reshape(frames * count, 27 * width)
    conv = jnp.dot(
        columns, conv_weight.reshape(27 * width, width), preferred_element_type=jnp.float32
    )
    return (mixed_wide + conv.reshape(features.shape)).astype(jnp.bfloat16)


def solution(mesh):
    sizes = dict(zip(mesh.axis_names, mesh.devices.shape))
    tile = sizes["tile"]
    y = 4
    z = 8
    x = tile // (y * z)
    fine = Mesh(mesh.devices.reshape(sizes["tm"], x, z, y), ("tm", *ROW_AXES))
    spec = P("tm", ROW_AXES, None, None)
    in_specs = (spec, P(), P(), P(), P(), P())
    return jax.shard_map(
        per_device, mesh=fine, in_specs=in_specs, out_specs=spec, check_vma=False
    )
```

```python
import math

import jax
import jax.numpy as jnp
from jax import lax
from jax.sharding import Mesh
from jax.sharding import PartitionSpec as P

ROW_AXES = ("x", "z", "y")


def rms_rows(values):
    return values * lax.rsqrt(jnp.mean(values * values, axis=-1, keepdims=True) + 1e-06)


def project(flat_rows, weight):
    return jnp.dot(flat_rows, weight, preferred_element_type=jnp.float32).astype(jnp.bfloat16)


def ring_shift(block, axis, step):
    n = lax.axis_size(axis)
    return lax.ppermute(block, axis, [(i, (i + step) % n) for i in range(n)])


def ring_gather(block, axis, split):
    n = lax.axis_size(axis)
    rel = [None] * n
    rel[0] = block
    right = left = block
    for s in range(1, n // 2):
        right = ring_shift(right, axis, 1)
        left = ring_shift(left, axis, -1)
        rel[n - s] = right
        rel[s] = left
    half = block.shape[split] // 2
    head = ring_shift(lax.slice_in_dim(right, 0, half, axis=split), axis, 1)
    tail = ring_shift(lax.slice_in_dim(left, half, block.shape[split], axis=split), axis, -1)
    rel[n // 2] = jnp.concatenate([head, tail], axis=split)
    return rel


def combine(first, second):
    high_a, total_a, summed_a = first
    high_b, total_b, summed_b = second
    fresh = jnp.maximum(high_a, high_b)
    weight_a = jnp.exp(high_a - fresh)
    weight_b = jnp.exp(high_b - fresh)
    total = total_a * weight_a + total_b * weight_b
    summed = summed_a * weight_a[..., None] + summed_b * weight_b[..., None]
    return fresh, total, summed


def ring_reduce(parts, axis, rows):
    n = lax.axis_size(axis)
    half = rows // 2

    def piece(k, lo, hi):
        high, total, summed = parts[k]
        return high[..., lo:hi], total[..., lo:hi], summed[..., lo:hi, :]

    def send(state, step):
        high, total, summed = state
        stats = jnp.stack([high, total])
        stats, summed = ring_shift((stats, summed.astype(jnp.bfloat16)), axis, step)
        return stats[0], stats[1], summed.astype(jnp.float32)

    right = piece(n - 1, 0, half)
    left = piece(1, half, rows)
    for s in range(1, n):
        right = combine(send(right, 1), piece((n - 1 - s) % n, 0, half))
        left = combine(send(left, -1), piece((s + 1) % n, half, rows))
    return tuple(jnp.concatenate([a, b], axis=-1 if a.ndim == 2 else -2) for a, b in zip(right, left))


def row_shift(block, forward):
    count = 1
    for name in ROW_AXES:
        count *= lax.axis_size(name)
    if forward:
        route = [(i, i + 1) for i in range(count - 1)]
    else:
        route = [(i + 1, i) for i in range(count - 1)]
    return lax.ppermute(block, ROW_AXES, route)


def per_device(features, query_weight, key_weight, value_weight, out_weight, conv_weight):
    frames, rows, cols, width = features.shape
    count = rows * cols
    widened = features.astype(jnp.float32)
    normed = rms_rows(widened).astype(jnp.bfloat16)
    flat = normed.reshape(frames * count, width)
    scale = 1.0 / math.sqrt(width)

    query = project(flat, query_weight).reshape(frames, count, width)
    query_rel = ring_gather(query, "z", 1)
    tokens = normed.reshape(frames, count, width)

    parts = []
    for frame in range(frames):
        first, second = ("y", "x") if frame % 2 == 0 else ("x", "y")
        inner = jnp.stack(ring_gather(tokens[frame], first, 0))
        outer = ring_gather(inner, second, 0)
        keys_in = jnp.concatenate(outer, axis=0).reshape(-1, width)
        key_rows = project(keys_in, key_weight)
        value_rows = project(keys_in, value_weight)
        query_rows = jnp.concatenate([q[frame] for q in query_rel], axis=0)
        scores = jnp.dot(query_rows, key_rows.T, preferred_element_type=jnp.float32) * scale
        highest = jnp.max(scores, axis=-1)
        expo = jnp.exp(scores - highest[:, None])
        total = jnp.sum(expo, axis=-1)
        summed = jnp.dot(expo.astype(jnp.bfloat16), value_rows, preferred_element_type=jnp.float32)
        parts.append((highest, total, summed))

    blocks = len(query_rel)
    by_offset = []
    for k in range(blocks):
        lo, hi = k * count, (k + 1) * count
        by_offset.append(
            tuple(jnp.stack([p[i][lo:hi] for p in parts]) for i in range(3))
        )
    _, total, summed = ring_reduce(by_offset, "z", count)
    attended = (summed / total[..., None]).astype(jnp.bfloat16)

    projected = jnp.dot(attended.reshape(-1, width), out_weight, preferred_element_type=jnp.float32)
    mixed = (widened + projected.reshape(features.shape)).astype(jnp.bfloat16)
    mixed_wide = mixed.astype(jnp.float32)
    activated = jax.nn.silu(rms_rows(mixed_wide)).astype(jnp.bfloat16)

    earlier = lax.ppermute(activated, "tm", [(0, 1)])
    stacked = jnp.concatenate([earlier, activated], axis=0)
    above = row_shift(stacked, True)
    below = row_shift(stacked, False)
    padded = jnp.concatenate([above, stacked, below], axis=1)
    padded = jnp.pad(padded, ((0, 0), (0, 0), (1, 1), (0, 0)))
    patches = []
    for tap_time in range(3):
        for tap_row in range(3):
            for tap_col in range(3):
                patches.append(
                    padded[
                        tap_time : tap_time + frames,
                        tap_row : tap_row + rows,
                        tap_col : tap_col + cols,
                    ]
                )
    columns = jnp.concatenate(patches, axis=-1).reshape(frames * count, 27 * width)
    conv = jnp.dot(
        columns, conv_weight.reshape(27 * width, width), preferred_element_type=jnp.float32
    )
    return (mixed_wide + conv.reshape(features.shape)).astype(jnp.bfloat16)


def solution(mesh):
    sizes = dict(zip(mesh.axis_names, mesh.devices.shape))
    tile = sizes["tile"]
    y = 4
    z = 8
    x = tile // (y * z)
    fine = Mesh(mesh.devices.reshape(sizes["tm"], x, z, y), ("tm", *ROW_AXES))
    spec = P("tm", ROW_AXES, None, None)
    in_specs = (spec, P(), P(), P(), P(), P())
    return jax.shard_map(
        per_device, mesh=fine, in_specs=in_specs, out_specs=spec, check_vma=False
    )
```

```python
import math

import jax
import jax.numpy as jnp
from jax import lax
from jax.sharding import Mesh
from jax.sharding import PartitionSpec as P

ROW_AXES = ("x", "z", "y")


def rms_rows(values):
    return values * lax.rsqrt(jnp.mean(values * values, axis=-1, keepdims=True) + 1e-06)


def project(flat_rows, weight):
    return jnp.dot(flat_rows, weight, preferred_element_type=jnp.float32).astype(jnp.bfloat16)


def ring_shift(block, axis, step):
    n = lax.axis_size(axis)
    return lax.ppermute(block, axis, [(i, (i + step) % n) for i in range(n)])


def ring_gather(block, axis, split):
    n = lax.axis_size(axis)
    rel = [None] * n
    rel[0] = block
    right = left = block
    for s in range(1, n // 2):
        right = ring_shift(right, axis, 1)
        left = ring_shift(left, axis, -1)
        rel[n - s] = right
        rel[s] = left
    half = block.shape[split] // 2
    head = ring_shift(lax.slice_in_dim(right, 0, half, axis=split), axis, 1)
    tail = ring_shift(lax.slice_in_dim(left, half, block.shape[split], axis=split), axis, -1)
    rel[n // 2] = jnp.concatenate([head, tail], axis=split)
    return rel


def combine(first, second):
    high_a, total_a, summed_a = first
    high_b, total_b, summed_b = second
    fresh = jnp.maximum(high_a, high_b)
    weight_a = jnp.exp(high_a - fresh)
    weight_b = jnp.exp(high_b - fresh)
    total = total_a * weight_a + total_b * weight_b
    summed = summed_a * weight_a[..., None] + summed_b * weight_b[..., None]
    return fresh, total, summed


def ring_reduce(parts, axis, rows):
    n = lax.axis_size(axis)
    half = rows // 2

    def piece(k, lo, hi):
        high, total, summed = parts[k]
        return high[..., lo:hi], total[..., lo:hi], summed[..., lo:hi, :]

    def send(state, step):
        high, total, summed = state
        stats = jnp.stack([high, total])
        stats, summed = ring_shift((stats, summed.astype(jnp.bfloat16)), axis, step)
        return stats[0], stats[1], summed.astype(jnp.float32)

    right = piece(n - 1, 0, half)
    left = piece(1, half, rows)
    for s in range(1, n):
        right = combine(send(right, 1), piece((n - 1 - s) % n, 0, half))
        left = combine(send(left, -1), piece((s + 1) % n, half, rows))
    return tuple(jnp.concatenate([a, b], axis=-1 if a.ndim == 2 else -2) for a, b in zip(right, left))


def row_shift(block, forward):
    count = 1
    for name in ROW_AXES:
        count *= lax.axis_size(name)
    if forward:
        route = [(i, i + 1) for i in range(count - 1)]
    else:
        route = [(i + 1, i) for i in range(count - 1)]
    return lax.ppermute(block, ROW_AXES, route)


def spread(block, axis, copies):
    wide = jnp.broadcast_to(block[None], (copies, *block.shape))
    return lax.all_to_all(wide, axis, 0, 0, tiled=False)


def per_device(features, query_weight, key_weight, value_weight, out_weight, conv_weight):
    frames, rows, cols, width = features.shape
    count = rows * cols
    widened = features.astype(jnp.float32)
    normed = rms_rows(widened).astype(jnp.bfloat16)
    flat = normed.reshape(frames * count, width)
    scale = 1.0 / math.sqrt(width)
    group_q = lax.axis_size("z")
    group_k = lax.axis_size("x") * lax.axis_size("y")

    query = project(flat, query_weight).reshape(frames, count, width)
    query_all = spread(query, "z", group_q)
    tokens_all = spread(normed.reshape(frames, count, width), ("x", "y"), group_k)
    keys_in = jnp.transpose(tokens_all, (1, 0, 2, 3)).reshape(-1, width)
    key_rows = project(keys_in, key_weight).reshape(frames, -1, width)
    value_rows = project(keys_in, value_weight).reshape(frames, -1, width)
    query_rows = jnp.transpose(query_all, (1, 0, 2, 3)).reshape(frames, -1, width)

    scores = jnp.einsum("fqd,fkd->fqk", query_rows, key_rows, preferred_element_type=jnp.float32) * scale
    highest = jnp.max(scores, axis=-1)
    expo = jnp.exp(scores - highest[..., None])
    total = jnp.sum(expo, axis=-1)
    summed = jnp.einsum("fqk,fkd->fqd", expo.astype(jnp.bfloat16), value_rows, preferred_element_type=jnp.float32)

    summed = jnp.transpose(summed.reshape(frames, group_q, count, width), (1, 0, 2, 3))
    stats = jnp.stack([highest, total], axis=1).reshape(frames, 2, group_q, count)
    stats = jnp.transpose(stats, (2, 0, 1, 3))
    summed = lax.all_to_all(summed.astype(jnp.bfloat16), "z", 0, 0, tiled=False)
    stats = lax.all_to_all(stats, "z", 0, 0, tiled=False)
    highest, total = stats[:, :, 0], stats[:, :, 1]
    fresh = jnp.max(highest, axis=0)
    weight = jnp.exp(highest - fresh[None])
    total = jnp.sum(total * weight, axis=0)
    summed = jnp.sum(summed.astype(jnp.float32) * weight[..., None], axis=0)
    attended = (summed / total[..., None]).astype(jnp.bfloat16)

    projected = jnp.dot(attended.reshape(-1, width), out_weight, preferred_element_type=jnp.float32)
    mixed = (widened + projected.reshape(features.shape)).astype(jnp.bfloat16)
    mixed_wide = mixed.astype(jnp.float32)
    activated = jax.nn.silu(rms_rows(mixed_wide)).astype(jnp.bfloat16)

    earlier = lax.ppermute(activated, "tm", [(0, 1)])
    stacked = jnp.concatenate([earlier, activated], axis=0)
    above = row_shift(stacked, True)
    below = row_shift(stacked, False)
    padded = jnp.concatenate([above, stacked, below], axis=1)
    padded = jnp.pad(padded, ((0, 0), (0, 0), (1, 1), (0, 0)))
    patches = []
    for tap_time in range(3):
        for tap_row in range(3):
            for tap_col in range(3):
                patches.append(
                    padded[
                        tap_time : tap_time + frames,
                        tap_row : tap_row + rows,
                        tap_col : tap_col + cols,
                    ]
                )
    columns = jnp.concatenate(patches, axis=-1).reshape(frames * count, 27 * width)
    conv = jnp.dot(
        columns, conv_weight.reshape(27 * width, width), preferred_element_type=jnp.float32
    )
    return (mixed_wide + conv.reshape(features.shape)).astype(jnp.bfloat16)


def solution(mesh):
    sizes = dict(zip(mesh.axis_names, mesh.devices.shape))
    tile = sizes["tile"]
    y = 4
    z = 8
    x = tile // (y * z)
    fine = Mesh(mesh.devices.reshape(sizes["tm"], x, z, y), ("tm", *ROW_AXES))
    spec = P("tm", ROW_AXES, None, None)
    in_specs = (spec, P(), P(), P(), P(), P())
    return jax.shard_map(
        per_device, mesh=fine, in_specs=in_specs, out_specs=spec, check_vma=False
    )
```

```python
import math

import jax
import jax.numpy as jnp
from jax import lax
from jax.sharding import Mesh
from jax.sharding import PartitionSpec as P

ROW_AXES = ("x", "z", "y")


def rms_rows(values):
    return values * lax.rsqrt(jnp.mean(values * values, axis=-1, keepdims=True) + 1e-06)


def project(flat_rows, weight):
    return jnp.dot(flat_rows, weight, preferred_element_type=jnp.float32).astype(jnp.bfloat16)


def ring_shift(block, axis, step):
    n = lax.axis_size(axis)
    return lax.ppermute(block, axis, [(i, (i + step) % n) for i in range(n)])


def ring_gather(block, axis):
    n = lax.axis_size(axis)
    rel = [None] * n
    rel[0] = block
    right = left = block
    for s in range(1, n // 2 + 1):
        right = ring_shift(right, axis, 1)
        rel[(n - s) % n] = right
    for s in range(1, n // 2):
        left = ring_shift(left, axis, -1)
        rel[s] = left
    return rel


def split3(values):
    hi = values.astype(jnp.bfloat16)
    rest = values - hi.astype(jnp.float32)
    mid = rest.astype(jnp.bfloat16)
    lo = (rest - mid.astype(jnp.float32)).astype(jnp.bfloat16)
    return [hi, mid, lo]


def join3(parts):
    hi, mid, lo = (p.astype(jnp.float32) for p in parts)
    return (hi + mid) + lo


def pack(state):
    high, total, summed = state
    frames, rows, width = summed.shape
    stats = jnp.stack(split3(high) + split3(total), axis=1).reshape(frames, -1, width)
    return jnp.concatenate([summed.astype(jnp.bfloat16), stats], axis=1)


def unpack(payload, rows):
    frames, _, width = payload.shape
    summed = payload[:, :rows].astype(jnp.float32)
    stats = payload[:, rows:].reshape(frames, 6, rows)
    high = join3([stats[:, 0], stats[:, 1], stats[:, 2]])
    total = join3([stats[:, 3], stats[:, 4], stats[:, 5]])
    return high, total, summed


def combine(first, second):
    high_a, total_a, summed_a = first
    high_b, total_b, summed_b = second
    fresh = jnp.maximum(high_a, high_b)
    weight_a = jnp.exp(high_a - fresh)
    weight_b = jnp.exp(high_b - fresh)
    total = total_a * weight_a + total_b * weight_b
    summed = summed_a * weight_a[..., None] + summed_b * weight_b[..., None]
    return fresh, total, summed


def ring_reduce(parts, axis, rows):
    n = lax.axis_size(axis)
    right_hops = n // 2
    left_hops = n - 1 - right_hops
    right = parts[right_hops]
    for s in range(1, right_hops + 1):
        right = unpack(ring_shift(pack(right), axis, 1), rows)
        if s < right_hops:
            right = combine(right, parts[right_hops - s])
    left = parts[(n - left_hops) % n]
    for s in range(1, left_hops + 1):
        left = unpack(ring_shift(pack(left), axis, -1), rows)
        if s < left_hops:
            left = combine(left, parts[(n - left_hops + s) % n])
    return combine(combine(right, left), parts[0])


def row_shift(block, forward):
    count = 1
    for name in ROW_AXES:
        count *= lax.axis_size(name)
    if forward:
        route = [(i, i + 1) for i in range(count - 1)]
    else:
        route = [(i + 1, i) for i in range(count - 1)]
    return lax.ppermute(block, ROW_AXES, route)


def per_device(features, query_weight, key_weight, value_weight, out_weight, conv_weight):
    frames, rows, cols, width = features.shape
    count = rows * cols
    widened = features.astype(jnp.float32)
    normed = rms_rows(widened).astype(jnp.bfloat16)
    flat = normed.reshape(frames * count, width)
    scale = 1.0 / math.sqrt(width)

    query = project(flat, query_weight).reshape(frames, count, width)
    query_rel = ring_gather(query, "z")
    inner = jnp.stack(ring_gather(normed.reshape(frames, count, width), "y"))
    outer = jnp.stack(ring_gather(inner, "x"))
    keys_in = jnp.transpose(outer, (2, 0, 1, 3, 4)).reshape(-1, width)
    key_rows = project(keys_in, key_weight).reshape(frames, -1, width)
    value_rows = project(keys_in, value_weight).reshape(frames, -1, width)
    query_rows = jnp.stack(query_rel, axis=1).reshape(frames, -1, width)

    scores = jnp.einsum("fqd,fkd->fqk", query_rows, key_rows, preferred_element_type=jnp.float32) * scale
    highest = jnp.max(scores, axis=-1)
    expo = jnp.exp(scores - highest[..., None])
    total = jnp.sum(expo, axis=-1)
    summed = jnp.einsum("fqk,fkd->fqd", expo.astype(jnp.bfloat16), value_rows, preferred_element_type=jnp.float32)

    parts = []
    for k in range(len(query_rel)):
        lo, hi = k * count, (k + 1) * count
        parts.append((highest[:, lo:hi], total[:, lo:hi], summed[:, lo:hi]))
    _, total, summed = ring_reduce(parts, "z", count)
    attended = (summed / total[..., None]).astype(jnp.bfloat16)

    projected = jnp.dot(attended.reshape(-1, width), out_weight, preferred_element_type=jnp.float32)
    mixed = (widened + projected.reshape(features.shape)).astype(jnp.bfloat16)
    mixed_wide = mixed.astype(jnp.float32)
    activated = jax.nn.silu(rms_rows(mixed_wide)).astype(jnp.bfloat16)

    earlier = lax.ppermute(activated, "tm", [(0, 1)])
    stacked = jnp.concatenate([earlier, activated], axis=0)
    above = row_shift(stacked, True)
    below = row_shift(stacked, False)
    padded = jnp.concatenate([above, stacked, below], axis=1)
    padded = jnp.pad(padded, ((0, 0), (0, 0), (1, 1), (0, 0)))
    patches = []
    for tap_time in range(3):
        for tap_row in range(3):
            for tap_col in range(3):
                patches.append(
                    padded[
                        tap_time : tap_time + frames,
                        tap_row : tap_row + rows,
                        tap_col : tap_col + cols,
                    ]
                )
    columns = jnp.concatenate(patches, axis=-1).reshape(frames * count, 27 * width)
    conv = jnp.dot(
        columns, conv_weight.reshape(27 * width, width), preferred_element_type=jnp.float32
    )
    return (mixed_wide + conv.reshape(features.shape)).astype(jnp.bfloat16)


def solution(mesh):
    sizes = dict(zip(mesh.axis_names, mesh.devices.shape))
    tile = sizes["tile"]
    y = 4
    z = 8
    x = tile // (y * z)
    fine = Mesh(mesh.devices.reshape(sizes["tm"], x, z, y), ("tm", *ROW_AXES))
    spec = P("tm", ROW_AXES, None, None)
    in_specs = (spec, P(), P(), P(), P(), P())
    return jax.shard_map(
        per_device, mesh=fine, in_specs=in_specs, out_specs=spec, check_vma=False
    )
```

```python
import functools
import math

import jax
import jax.numpy as jnp
from jax import lax
from jax.experimental import pallas as pl
from jax.experimental.pallas import tpu as pltpu
from jax.sharding import Mesh
from jax.sharding import PartitionSpec as P

ROW_AXES = ("x", "z", "y")


def rms_rows(values):
    return values * lax.rsqrt(jnp.mean(values * values, axis=-1, keepdims=True) + 1e-06)


def project(flat_rows, weight):
    return jnp.dot(flat_rows, weight, preferred_element_type=jnp.float32).astype(jnp.bfloat16)


def ring_shift(block, axis, step):
    n = lax.axis_size(axis)
    return lax.ppermute(block, axis, [(i, (i + step) % n) for i in range(n)])


def ring_gather(block, axis):
    n = lax.axis_size(axis)
    rel = [None] * n
    rel[0] = block
    right = left = block
    for s in range(1, n // 2 + 1):
        right = ring_shift(right, axis, 1)
        rel[(n - s) % n] = right
    for s in range(1, n // 2):
        left = ring_shift(left, axis, -1)
        rel[s] = left
    return rel


def split3(values):
    hi = values.astype(jnp.bfloat16)
    rest = values - hi.astype(jnp.float32)
    mid = rest.astype(jnp.bfloat16)
    lo = (rest - mid.astype(jnp.float32)).astype(jnp.bfloat16)
    return [hi, mid, lo]


def join3(parts):
    hi, mid, lo = (p.astype(jnp.float32) for p in parts)
    return (hi + mid) + lo


def pack(state):
    high, total, summed = state
    frames, rows, width = summed.shape
    stats = jnp.stack(split3(high) + split3(total), axis=1).reshape(frames, -1, width)
    return jnp.concatenate([summed.astype(jnp.bfloat16), stats], axis=1)


def unpack(payload, rows):
    frames, _, width = payload.shape
    summed = payload[:, :rows].astype(jnp.float32)
    stats = payload[:, rows:].reshape(frames, 6, rows)
    high = join3([stats[:, 0], stats[:, 1], stats[:, 2]])
    total = join3([stats[:, 3], stats[:, 4], stats[:, 5]])
    return high, total, summed


def combine(first, second):
    high_a, total_a, summed_a = first
    high_b, total_b, summed_b = second
    fresh = jnp.maximum(high_a, high_b)
    weight_a = jnp.exp(high_a - fresh)
    weight_b = jnp.exp(high_b - fresh)
    total = total_a * weight_a + total_b * weight_b
    summed = summed_a * weight_a[..., None] + summed_b * weight_b[..., None]
    return fresh, total, summed


def ring_reduce(parts, axis, rows):
    n = lax.axis_size(axis)
    right_hops = n // 2
    left_hops = n - 1 - right_hops
    right = parts[right_hops]
    for s in range(1, right_hops + 1):
        right = unpack(ring_shift(pack(right), axis, 1), rows)
        if s < right_hops:
            right = combine(right, parts[right_hops - s])
    left = parts[(n - left_hops) % n]
    for s in range(1, left_hops + 1):
        left = unpack(ring_shift(pack(left), axis, -1), rows)
        if s < left_hops:
            left = combine(left, parts[(n - left_hops + s) % n])
    return combine(combine(right, left), parts[0])


def row_shift(block, forward):
    count = 1
    for name in ROW_AXES:
        count *= lax.axis_size(name)
    if forward:
        route = [(i, i + 1) for i in range(count - 1)]
    else:
        route = [(i + 1, i) for i in range(count - 1)]
    return lax.ppermute(block, ROW_AXES, route)


def attention_kernel(scale, query_ref, key_ref, value_ref, high_ref, total_ref, summed_ref):
    scores = lax.dot_general(
        query_ref[0], key_ref[0], (((1,), (1,)), ((), ())), preferred_element_type=jnp.float32
    ) * scale
    high = jnp.max(scores, axis=-1, keepdims=True)
    expo = jnp.exp(scores - high)
    high_ref[0] = high
    total_ref[0] = jnp.sum(expo, axis=-1, keepdims=True)
    summed_ref[0] = jnp.dot(expo.astype(jnp.bfloat16), value_ref[0], preferred_element_type=jnp.float32)


def attention(query_rows, key_rows, value_rows):
    frames, queries, width = query_rows.shape
    keys = key_rows.shape[1]
    tile = 256
    scale = 1.0 / math.sqrt(width)
    stat = jax.ShapeDtypeStruct((frames, queries, 1), jnp.float32)
    return pl.pallas_call(
        functools.partial(attention_kernel, scale),
        grid=(frames, queries // tile),
        in_specs=[
            pl.BlockSpec((1, tile, width), lambda f, i: (f, i, 0)),
            pl.BlockSpec((1, keys, width), lambda f, i: (f, 0, 0)),
            pl.BlockSpec((1, keys, width), lambda f, i: (f, 0, 0)),
        ],
        out_specs=[
            pl.BlockSpec((1, tile, 1), lambda f, i: (f, i, 0)),
            pl.BlockSpec((1, tile, 1), lambda f, i: (f, i, 0)),
            pl.BlockSpec((1, tile, width), lambda f, i: (f, i, 0)),
        ],
        out_shape=[stat, stat, jax.ShapeDtypeStruct((frames, queries, width), jnp.float32)],
        cost_estimate=pl.CostEstimate(
            flops=4 * frames * queries * keys * width,
            transcendentals=frames * queries * keys,
            bytes_accessed=2 * frames * (queries + 2 * keys) * width + 4 * frames * queries * width,
        ),
    )(query_rows, key_rows, value_rows)


def per_device(features, query_weight, key_weight, value_weight, out_weight, conv_weight):
    frames, rows, cols, width = features.shape
    count = rows * cols
    widened = features.astype(jnp.float32)
    normed = rms_rows(widened).astype(jnp.bfloat16)
    flat = normed.reshape(frames * count, width)
    scale = 1.0 / math.sqrt(width)

    query = project(flat, query_weight).reshape(frames, count, width)
    query_rel = ring_gather(query, "z")
    inner = jnp.stack(ring_gather(normed.reshape(frames, count, width), "y"))
    outer = jnp.stack(ring_gather(inner, "x"))
    keys_in = jnp.transpose(outer, (2, 0, 1, 3, 4)).reshape(-1, width)
    key_rows = project(keys_in, key_weight).reshape(frames, -1, width)
    value_rows = project(keys_in, value_weight).reshape(frames, -1, width)
    query_rows = jnp.stack(query_rel, axis=1).reshape(frames, -1, width)

    highest, total, summed = attention(query_rows, key_rows, value_rows)
    highest, total = highest[..., 0], total[..., 0]

    parts = []
    for k in range(len(query_rel)):
        lo, hi = k * count, (k + 1) * count
        parts.append((highest[:, lo:hi], total[:, lo:hi], summed[:, lo:hi]))
    _, total, summed = ring_reduce(parts, "z", count)
    attended = (summed / total[..., None]).astype(jnp.bfloat16)

    projected = jnp.dot(attended.reshape(-1, width), out_weight, preferred_element_type=jnp.float32)
    mixed = (widened + projected.reshape(features.shape)).astype(jnp.bfloat16)
    mixed_wide = mixed.astype(jnp.float32)
    activated = jax.nn.silu(rms_rows(mixed_wide)).astype(jnp.bfloat16)

    earlier = lax.ppermute(activated, "tm", [(0, 1)])
    stacked = jnp.concatenate([earlier, activated], axis=0)
    above = row_shift(stacked, True)
    below = row_shift(stacked, False)
    padded = jnp.concatenate([above, stacked, below], axis=1)
    padded = jnp.pad(padded, ((0, 0), (0, 0), (1, 1), (0, 0)))
    patches = []
    for tap_time in range(3):
        for tap_row in range(3):
            for tap_col in range(3):
                patches.append(
                    padded[
                        tap_time : tap_time + frames,
                        tap_row : tap_row + rows,
                        tap_col : tap_col + cols,
                    ]
                )
    columns = jnp.concatenate(patches, axis=-1).reshape(frames * count, 27 * width)
    conv = jnp.dot(
        columns, conv_weight.reshape(27 * width, width), preferred_element_type=jnp.float32
    )
    return (mixed_wide + conv.reshape(features.shape)).astype(jnp.bfloat16)


def solution(mesh):
    sizes = dict(zip(mesh.axis_names, mesh.devices.shape))
    tile = sizes["tile"]
    y = 4
    z = 8
    x = tile // (y * z)
    fine = Mesh(mesh.devices.reshape(sizes["tm"], x, z, y), ("tm", *ROW_AXES))
    spec = P("tm", ROW_AXES, None, None)
    in_specs = (spec, P(), P(), P(), P(), P())
    return jax.shard_map(
        per_device, mesh=fine, in_specs=in_specs, out_specs=spec, check_vma=False
    )
```

```python
import functools
import math

import jax
import jax.numpy as jnp
from jax import lax
from jax.experimental import pallas as pl
from jax.experimental.pallas import tpu as pltpu
from jax.sharding import Mesh
from jax.sharding import PartitionSpec as P

ROW_AXES = ("x", "z", "y")


def rms_rows(values):
    return values * lax.rsqrt(jnp.mean(values * values, axis=-1, keepdims=True) + 1e-06)


def project(flat_rows, weight):
    return jnp.dot(flat_rows, weight, preferred_element_type=jnp.float32).astype(jnp.bfloat16)


def ring_shift(block, axis, step):
    n = lax.axis_size(axis)
    return lax.ppermute(block, axis, [(i, (i + step) % n) for i in range(n)])


def ring_gather(block, axis, halve=False):
    n = lax.axis_size(axis)
    rel = [None] * n
    rel[0] = block
    right = left = block
    for s in range(1, n // 2):
        right = ring_shift(right, axis, 1)
        rel[n - s] = right
        left = ring_shift(left, axis, -1)
        rel[s] = left
    if halve:
        half = block.shape[0] // 2
        head = ring_shift(right[:half], axis, 1)
        tail = ring_shift(left[half:], axis, -1)
        rel[n // 2] = jnp.concatenate([head, tail], axis=0)
    else:
        rel[n // 2] = ring_shift(right, axis, 1)
    return rel


def split3(values):
    hi = values.astype(jnp.bfloat16)
    rest = values - hi.astype(jnp.float32)
    mid = rest.astype(jnp.bfloat16)
    lo = (rest - mid.astype(jnp.float32)).astype(jnp.bfloat16)
    return [hi, mid, lo]


def join3(parts):
    hi, mid, lo = (p.astype(jnp.float32) for p in parts)
    return (hi + mid) + lo


def pack(state):
    high, total, summed = state
    frames, rows, width = summed.shape
    stats = jnp.stack(split3(high) + split3(total), axis=1).reshape(frames, -1, width)
    return jnp.concatenate([summed.astype(jnp.bfloat16), stats], axis=1)


def unpack(payload, rows):
    frames, _, width = payload.shape
    summed = payload[:, :rows].astype(jnp.float32)
    stats = payload[:, rows:].reshape(frames, 6, rows)
    high = join3([stats[:, 0], stats[:, 1], stats[:, 2]])
    total = join3([stats[:, 3], stats[:, 4], stats[:, 5]])
    return high, total, summed


def combine(first, second):
    high_a, total_a, summed_a = first
    high_b, total_b, summed_b = second
    fresh = jnp.maximum(high_a, high_b)
    weight_a = jnp.exp(high_a - fresh)
    weight_b = jnp.exp(high_b - fresh)
    total = total_a * weight_a + total_b * weight_b
    summed = summed_a * weight_a[..., None] + summed_b * weight_b[..., None]
    return fresh, total, summed


def ring_reduce(parts, axis, rows):
    n = lax.axis_size(axis)
    right_hops = n // 2
    left_hops = n - 1 - right_hops
    right = parts[right_hops]
    for s in range(1, right_hops + 1):
        right = unpack(ring_shift(pack(right), axis, 1), rows)
        if s < right_hops:
            right = combine(right, parts[right_hops - s])
    left = parts[(n - left_hops) % n]
    for s in range(1, left_hops + 1):
        left = unpack(ring_shift(pack(left), axis, -1), rows)
        if s < left_hops:
            left = combine(left, parts[(n - left_hops + s) % n])
    return combine(combine(right, left), parts[0])


def row_shift(block, forward):
    count = 1
    for name in ROW_AXES:
        count *= lax.axis_size(name)
    if forward:
        route = [(i, i + 1) for i in range(count - 1)]
    else:
        route = [(i + 1, i) for i in range(count - 1)]
    return lax.ppermute(block, ROW_AXES, route)


def attention_kernel(scale, query_ref, key_ref, value_ref, high_ref, total_ref, summed_ref, short_ref):
    scores = lax.dot_general(
        query_ref[0], key_ref[0], (((1,), (1,)), ((), ())), preferred_element_type=jnp.float32
    ) * scale
    high = jnp.max(scores, axis=-1, keepdims=True)
    expo = jnp.exp(scores - high)
    total = jnp.sum(expo, axis=-1, keepdims=True)
    rows = high.shape[0]
    high_ref[0] = jnp.transpose(jnp.broadcast_to(high, (rows, 128)))[0:1, :]
    total_ref[0] = jnp.transpose(jnp.broadcast_to(total, (rows, 128)))[0:1, :]
    summed = jnp.dot(expo.astype(jnp.bfloat16), value_ref[0], preferred_element_type=jnp.float32)
    summed_ref[0] = summed
    short_ref[0] = summed.astype(jnp.bfloat16)


def attention(query_rows, key_rows, value_rows):
    frames, queries, width = query_rows.shape
    keys = key_rows.shape[1]
    tile = 256
    scale = 1.0 / math.sqrt(width)
    stat = jax.ShapeDtypeStruct((frames, 1, queries), jnp.float32)
    stat_spec = pl.BlockSpec((1, 1, tile), lambda f, i: (f, 0, i))
    row_spec = pl.BlockSpec((1, tile, width), lambda f, i: (f, i, 0))
    return pl.pallas_call(
        functools.partial(attention_kernel, scale),
        grid=(frames, queries // tile),
        in_specs=[
            row_spec,
            pl.BlockSpec((1, keys, width), lambda f, i: (f, 0, 0)),
            pl.BlockSpec((1, keys, width), lambda f, i: (f, 0, 0)),
        ],
        out_specs=[stat_spec, stat_spec, row_spec, row_spec],
        out_shape=[
            stat,
            stat,
            jax.ShapeDtypeStruct((frames, queries, width), jnp.float32),
            jax.ShapeDtypeStruct((frames, queries, width), jnp.bfloat16),
        ],
        cost_estimate=pl.CostEstimate(
            flops=4 * frames * queries * keys * width,
            transcendentals=frames * queries * keys,
            bytes_accessed=2 * frames * (queries + 2 * keys) * width + 6 * frames * queries * width,
        ),
    )(query_rows, key_rows, value_rows)


def per_device(features, query_weight, key_weight, value_weight, out_weight, conv_weight):
    frames, rows, cols, width = features.shape
    count = rows * cols
    widened = features.astype(jnp.float32)
    normed = rms_rows(widened).astype(jnp.bfloat16)
    flat = normed.reshape(frames * count, width)
    scale = 1.0 / math.sqrt(width)

    query = project(flat, query_weight).reshape(frames, count, width)
    query_rel = ring_gather(query, "z")
    inner = jnp.stack(ring_gather(normed.reshape(frames, count, width), "y"))
    outer = jnp.stack(ring_gather(inner, "x", halve=True))
    keys_in = jnp.transpose(outer, (2, 0, 1, 3, 4)).reshape(-1, width)
    key_rows = project(keys_in, key_weight).reshape(frames, -1, width)
    value_rows = project(keys_in, value_weight).reshape(frames, -1, width)
    query_rows = jnp.stack(query_rel, axis=1).reshape(frames, -1, width)

    highest, total, summed, short = attention(query_rows, key_rows, value_rows)
    highest, total = highest[:, 0], total[:, 0]

    blocks = len(query_rel)
    first_sent = (blocks // 2, (blocks + 1) // 2 + 1)
    parts = []
    for k in range(blocks):
        lo, hi = k * count, (k + 1) * count
        rows_of = short if k in first_sent else summed
        parts.append((highest[:, lo:hi], total[:, lo:hi], rows_of[:, lo:hi]))
    _, total, summed = ring_reduce(parts, "z", count)
    attended = (summed / total[..., None]).astype(jnp.bfloat16)

    projected = jnp.dot(attended.reshape(-1, width), out_weight, preferred_element_type=jnp.float32)
    mixed = (widened + projected.reshape(features.shape)).astype(jnp.bfloat16)
    mixed_wide = mixed.astype(jnp.float32)
    activated = jax.nn.silu(rms_rows(mixed_wide)).astype(jnp.bfloat16)

    every = ("tm", *ROW_AXES)
    count_rows = 1
    for name in ROW_AXES:
        count_rows *= lax.axis_size(name)
    earlier = lax.ppermute(activated, "tm", [(0, 1)])
    earlier_above = lax.ppermute(activated, every, [(r, count_rows + r + 1) for r in range(count_rows - 1)])
    earlier_below = lax.ppermute(activated, every, [(r + 1, count_rows + r) for r in range(count_rows - 1)])
    above = jnp.concatenate([earlier_above, row_shift(activated, True)], axis=0)
    below = jnp.concatenate([earlier_below, row_shift(activated, False)], axis=0)
    stacked = jnp.concatenate([earlier, activated], axis=0)
    padded = jnp.concatenate([above, stacked, below], axis=1)
    padded = jnp.pad(padded, ((0, 0), (0, 0), (1, 1), (0, 0)))
    patches = []
    for tap_time in range(3):
        for tap_row in range(3):
            for tap_col in range(3):
                patches.append(
                    padded[
                        tap_time : tap_time + frames,
                        tap_row : tap_row + rows,
                        tap_col : tap_col + cols,
                    ]
                )
    columns = jnp.concatenate(patches, axis=-1).reshape(frames * count, 27 * width)
    conv = jnp.dot(
        columns, conv_weight.reshape(27 * width, width), preferred_element_type=jnp.float32
    )
    return (mixed_wide + conv.reshape(features.shape)).astype(jnp.bfloat16)


def solution(mesh):
    sizes = dict(zip(mesh.axis_names, mesh.devices.shape))
    tile = sizes["tile"]
    y = 4
    z = 8
    x = tile // (y * z)
    fine = Mesh(mesh.devices.reshape(sizes["tm"], x, z, y), ("tm", *ROW_AXES))
    spec = P("tm", ROW_AXES, None, None)
    in_specs = (spec, P(), P(), P(), P(), P())
    return jax.shard_map(
        per_device, mesh=fine, in_specs=in_specs, out_specs=spec, check_vma=False
    )
```

```python
import functools
import math

import jax
import jax.numpy as jnp
from jax import lax
from jax.experimental import pallas as pl
from jax.experimental.pallas import tpu as pltpu
from jax.sharding import Mesh
from jax.sharding import PartitionSpec as P

ROW_AXES = ("x", "z", "y")


def rms_rows(values):
    return values * lax.rsqrt(jnp.mean(values * values, axis=-1, keepdims=True) + 1e-06)


def project(flat_rows, weight):
    return jnp.dot(flat_rows, weight, preferred_element_type=jnp.float32).astype(jnp.bfloat16)


def ring_shift(block, axis, step):
    n = lax.axis_size(axis)
    return lax.ppermute(block, axis, [(i, (i + step) % n) for i in range(n)])


def ring_gather(block, axis, halve=False):
    n = lax.axis_size(axis)
    rel = [None] * n
    rel[0] = block
    right = left = block
    for s in range(1, n // 2):
        right = ring_shift(right, axis, 1)
        rel[n - s] = right
        left = ring_shift(left, axis, -1)
        rel[s] = left
    if halve:
        half = block.shape[0] // 2
        head = ring_shift(right[:half], axis, 1)
        tail = ring_shift(left[half:], axis, -1)
        rel[n // 2] = jnp.concatenate([head, tail], axis=0)
    else:
        rel[n // 2] = ring_shift(right, axis, 1)
    return rel


def split3(values):
    hi = values.astype(jnp.bfloat16)
    rest = values - hi.astype(jnp.float32)
    mid = rest.astype(jnp.bfloat16)
    lo = (rest - mid.astype(jnp.float32)).astype(jnp.bfloat16)
    return [hi, mid, lo]


def join3(parts):
    hi, mid, lo = (p.astype(jnp.float32) for p in parts)
    return (hi + mid) + lo


def pack(state):
    high, total, summed = state
    frames, rows, width = summed.shape
    stats = jnp.stack(split3(high) + split3(total), axis=1).reshape(frames, -1, width)
    return jnp.concatenate([summed.astype(jnp.bfloat16), stats], axis=1)


def unpack(payload, rows):
    frames, _, width = payload.shape
    summed = payload[:, :rows].astype(jnp.float32)
    stats = payload[:, rows:].reshape(frames, 6, rows)
    high = join3([stats[:, 0], stats[:, 1], stats[:, 2]])
    total = join3([stats[:, 3], stats[:, 4], stats[:, 5]])
    return high, total, summed


def combine(first, second):
    high_a, total_a, summed_a = first
    high_b, total_b, summed_b = second
    fresh = jnp.maximum(high_a, high_b)
    weight_a = jnp.exp(high_a - fresh)
    weight_b = jnp.exp(high_b - fresh)
    total = total_a * weight_a + total_b * weight_b
    summed = summed_a * weight_a[..., None] + summed_b * weight_b[..., None]
    return fresh, total, summed


def ring_reduce(parts, axis, rows):
    n = lax.axis_size(axis)
    right_hops = n // 2
    left_hops = n - 1 - right_hops
    right = parts[right_hops]
    for s in range(1, right_hops + 1):
        right = unpack(ring_shift(pack(right), axis, 1), rows)
        if s < right_hops:
            right = combine(right, parts[right_hops - s])
    left = parts[(n - left_hops) % n]
    for s in range(1, left_hops + 1):
        left = unpack(ring_shift(pack(left), axis, -1), rows)
        if s < left_hops:
            left = combine(left, parts[(n - left_hops + s) % n])
    return combine(combine(right, left), parts[0])


def row_shift(block, forward):
    count = 1
    for name in ROW_AXES:
        count *= lax.axis_size(name)
    if forward:
        route = [(i, i + 1) for i in range(count - 1)]
    else:
        route = [(i + 1, i) for i in range(count - 1)]
    return lax.ppermute(block, ROW_AXES, route)


def attention_kernel(
    scale, query_ref, token_ref, key_w_ref, value_w_ref,
    high_ref, total_ref, summed_ref, short_ref, key_scr, value_scr,
):
    width = key_scr.shape[-1]

    @pl.when(pl.program_id(1) == 0)
    def _():
        tokens = token_ref[...].reshape(-1, width)
        key_scr[...] = jnp.dot(tokens, key_w_ref[...], preferred_element_type=jnp.float32).astype(jnp.bfloat16)
        value_scr[...] = jnp.dot(tokens, value_w_ref[...], preferred_element_type=jnp.float32).astype(jnp.bfloat16)

    query = query_ref[...].reshape(-1, width)
    scores = lax.dot_general(
        query, key_scr[...], (((1,), (1,)), ((), ())), preferred_element_type=jnp.float32
    ) * scale
    high = jnp.max(scores, axis=-1, keepdims=True)
    expo = jnp.exp(scores - high)
    total = jnp.sum(expo, axis=-1, keepdims=True)
    rows = high.shape[0]
    high_ref[0] = jnp.transpose(jnp.broadcast_to(high, (rows, 128)))[0:1, :]
    total_ref[0] = jnp.transpose(jnp.broadcast_to(total, (rows, 128)))[0:1, :]
    summed = jnp.dot(expo.astype(jnp.bfloat16), value_scr[...], preferred_element_type=jnp.float32)
    summed_ref[0] = summed
    short_ref[0] = summed.astype(jnp.bfloat16)


def attention(query_blocks, token_blocks, key_weight, value_weight):
    query_count, frames, rows, width = query_blocks.shape
    key_count = token_blocks.shape[0]
    per_tile = 2
    tile = per_tile * rows
    queries = query_count * rows
    scale = 1.0 / math.sqrt(width)
    stat = jax.ShapeDtypeStruct((frames, 1, queries), jnp.float32)
    stat_spec = pl.BlockSpec((1, 1, tile), lambda f, i: (f, 0, i))
    row_spec = pl.BlockSpec((1, tile, width), lambda f, i: (f, i, 0))
    weight_spec = pl.BlockSpec((width, width), lambda f, i: (0, 0))
    keys = key_count * rows
    return pl.pallas_call(
        functools.partial(attention_kernel, scale),
        grid=(frames, query_count // per_tile),
        in_specs=[
            pl.BlockSpec((per_tile, None, rows, width), lambda f, i: (i, f, 0, 0)),
            pl.BlockSpec((key_count, None, rows, width), lambda f, i: (0, f, 0, 0)),
            weight_spec,
            weight_spec,
        ],
        out_specs=[stat_spec, stat_spec, row_spec, row_spec],
        out_shape=[
            stat,
            stat,
            jax.ShapeDtypeStruct((frames, queries, width), jnp.float32),
            jax.ShapeDtypeStruct((frames, queries, width), jnp.bfloat16),
        ],
        scratch_shapes=[
            pltpu.VMEM((keys, width), jnp.bfloat16),
            pltpu.VMEM((keys, width), jnp.bfloat16),
        ],
        cost_estimate=pl.CostEstimate(
            flops=4 * frames * queries * keys * width + 4 * frames * keys * width * width,
            transcendentals=frames * queries * keys,
            bytes_accessed=2 * frames * (queries + keys) * width + 6 * frames * queries * width,
        ),
    )(query_blocks, token_blocks, key_weight, value_weight)


def per_device(features, query_weight, key_weight, value_weight, out_weight, conv_weight):
    frames, rows, cols, width = features.shape
    count = rows * cols
    widened = features.astype(jnp.float32)
    normed = rms_rows(widened).astype(jnp.bfloat16)
    flat = normed.reshape(frames * count, width)
    scale = 1.0 / math.sqrt(width)

    query = project(flat, query_weight).reshape(frames, count, width)
    query_rel = ring_gather(query, "z")
    inner = jnp.stack(ring_gather(normed.reshape(frames, count, width), "y"))
    outer = jnp.stack(ring_gather(inner, "x", halve=True))
    token_blocks = outer.reshape(-1, *outer.shape[2:])
    query_blocks = jnp.stack(query_rel)
    highest, total, summed, short = attention(query_blocks, token_blocks, key_weight, value_weight)
    highest, total = highest[:, 0], total[:, 0]

    blocks = len(query_rel)
    first_sent = (blocks // 2, (blocks + 1) // 2 + 1)
    parts = []
    for k in range(blocks):
        lo, hi = k * count, (k + 1) * count
        rows_of = short if k in first_sent else summed
        parts.append((highest[:, lo:hi], total[:, lo:hi], rows_of[:, lo:hi]))
    _, total, summed = ring_reduce(parts, "z", count)
    attended = (summed / total[..., None]).astype(jnp.bfloat16)

    projected = jnp.dot(attended.reshape(-1, width), out_weight, preferred_element_type=jnp.float32)
    mixed = (widened + projected.reshape(features.shape)).astype(jnp.bfloat16)
    mixed_wide = mixed.astype(jnp.float32)
    activated = jax.nn.silu(rms_rows(mixed_wide)).astype(jnp.bfloat16)

    every = ("tm", *ROW_AXES)
    count_rows = 1
    for name in ROW_AXES:
        count_rows *= lax.axis_size(name)
    earlier = lax.ppermute(activated, "tm", [(0, 1)])
    earlier_above = lax.ppermute(activated, every, [(r, count_rows + r + 1) for r in range(count_rows - 1)])
    earlier_below = lax.ppermute(activated, every, [(r + 1, count_rows + r) for r in range(count_rows - 1)])
    above = jnp.concatenate([earlier_above, row_shift(activated, True)], axis=0)
    below = jnp.concatenate([earlier_below, row_shift(activated, False)], axis=0)
    stacked = jnp.concatenate([earlier, activated], axis=0)
    padded = jnp.concatenate([above, stacked, below], axis=1)
    padded = jnp.pad(padded, ((0, 0), (0, 0), (1, 1), (0, 0)))
    patches = []
    for tap_time in range(3):
        for tap_row in range(3):
            for tap_col in range(3):
                patches.append(
                    padded[
                        tap_time : tap_time + frames,
                        tap_row : tap_row + rows,
                        tap_col : tap_col + cols,
                    ]
                )
    columns = jnp.concatenate(patches, axis=-1).reshape(frames * count, 27 * width)
    conv = jnp.dot(
        columns, conv_weight.reshape(27 * width, width), preferred_element_type=jnp.float32
    )
    return (mixed_wide + conv.reshape(features.shape)).astype(jnp.bfloat16)


def solution(mesh):
    sizes = dict(zip(mesh.axis_names, mesh.devices.shape))
    tile = sizes["tile"]
    y = 4
    z = 8
    x = tile // (y * z)
    fine = Mesh(mesh.devices.reshape(sizes["tm"], x, z, y), ("tm", *ROW_AXES))
    spec = P("tm", ROW_AXES, None, None)
    in_specs = (spec, P(), P(), P(), P(), P())
    return jax.shard_map(
        per_device, mesh=fine, in_specs=in_specs, out_specs=spec, check_vma=False
    )
```

```python
import functools
import math

import jax
import jax.numpy as jnp
from jax import lax
from jax.experimental import pallas as pl
from jax.experimental.pallas import tpu as pltpu
from jax.sharding import Mesh
from jax.sharding import PartitionSpec as P

ROW_AXES = ("x", "z", "y")


def rms_rows(values):
    return values * lax.rsqrt(jnp.mean(values * values, axis=-1, keepdims=True) + 1e-06)


def project(flat_rows, weight):
    return jnp.dot(flat_rows, weight, preferred_element_type=jnp.float32).astype(jnp.bfloat16)


def ring_shift(block, axis, step):
    n = lax.axis_size(axis)
    return lax.ppermute(block, axis, [(i, (i + step) % n) for i in range(n)])


def ring_gather(block, axis, halve=False):
    n = lax.axis_size(axis)
    rel = [None] * n
    rel[0] = block
    right = left = block
    for s in range(1, n // 2):
        right = ring_shift(right, axis, 1)
        rel[n - s] = right
        left = ring_shift(left, axis, -1)
        rel[s] = left
    if halve:
        half = block.shape[0] // 2
        head = ring_shift(right[:half], axis, 1)
        tail = ring_shift(left[half:], axis, -1)
        rel[n // 2] = jnp.concatenate([head, tail], axis=0)
    else:
        rel[n // 2] = ring_shift(right, axis, 1)
    return rel


def split3(values):
    hi = values.astype(jnp.bfloat16)
    rest = values - hi.astype(jnp.float32)
    mid = rest.astype(jnp.bfloat16)
    lo = (rest - mid.astype(jnp.float32)).astype(jnp.bfloat16)
    return [hi, mid, lo]


def join3(parts):
    hi, mid, lo = (p.astype(jnp.float32) for p in parts)
    return (hi + mid) + lo


def pack(state):
    high, total, summed = state
    frames, rows, width = summed.shape
    stats = jnp.stack(split3(high) + split3(total), axis=1).reshape(frames, -1, width)
    return jnp.concatenate([summed.astype(jnp.bfloat16), stats], axis=1)


def unpack(payload, rows):
    frames, _, width = payload.shape
    summed = payload[:, :rows].astype(jnp.float32)
    stats = payload[:, rows:].reshape(frames, 6, rows)
    high = join3([stats[:, 0], stats[:, 1], stats[:, 2]])
    total = join3([stats[:, 3], stats[:, 4], stats[:, 5]])
    return high, total, summed


def combine(first, second):
    high_a, total_a, summed_a = first
    high_b, total_b, summed_b = second
    fresh = jnp.maximum(high_a, high_b)
    weight_a = jnp.exp(high_a - fresh)
    weight_b = jnp.exp(high_b - fresh)
    total = total_a * weight_a + total_b * weight_b
    summed = summed_a * weight_a[..., None] + summed_b * weight_b[..., None]
    return fresh, total, summed


def ring_reduce(parts, axis, rows):
    n = lax.axis_size(axis)
    right_hops = n // 2
    left_hops = n - 1 - right_hops
    right = parts[right_hops]
    for s in range(1, right_hops + 1):
        right = unpack(ring_shift(pack(right), axis, 1), rows)
        if s < right_hops:
            right = combine(right, parts[right_hops - s])
    left = parts[(n - left_hops) % n]
    for s in range(1, left_hops + 1):
        left = unpack(ring_shift(pack(left), axis, -1), rows)
        if s < left_hops:
            left = combine(left, parts[(n - left_hops + s) % n])
    return combine(combine(right, left), parts[0])


def row_shift(block, forward):
    count = 1
    for name in ROW_AXES:
        count *= lax.axis_size(name)
    if forward:
        route = [(i, i + 1) for i in range(count - 1)]
    else:
        route = [(i + 1, i) for i in range(count - 1)]
    return lax.ppermute(block, ROW_AXES, route)


def projection_kernel(token_ref, key_w_ref, value_w_ref, key_ref, value_ref):
    width = key_ref.shape[-1]
    tokens = token_ref[...].reshape(-1, width)
    key_ref[0] = jnp.dot(tokens, key_w_ref[...], preferred_element_type=jnp.float32).astype(jnp.bfloat16)
    value_ref[0] = jnp.dot(tokens, value_w_ref[...], preferred_element_type=jnp.float32).astype(jnp.bfloat16)


def project_keys(token_blocks, key_weight, value_weight):
    key_count, frames, rows, width = token_blocks.shape
    keys = key_count * rows
    weight_spec = pl.BlockSpec((width, width), lambda f: (0, 0))
    out_spec = pl.BlockSpec((1, keys, width), lambda f: (f, 0, 0))
    shape = jax.ShapeDtypeStruct((frames, keys, width), jnp.bfloat16)
    return pl.pallas_call(
        projection_kernel,
        grid=(frames,),
        in_specs=[
            pl.BlockSpec((key_count, None, rows, width), lambda f: (0, f, 0, 0)),
            weight_spec,
            weight_spec,
        ],
        out_specs=[out_spec, out_spec],
        out_shape=[shape, shape],
        cost_estimate=pl.CostEstimate(
            flops=4 * frames * keys * width * width,
            transcendentals=0,
            bytes_accessed=6 * frames * keys * width,
        ),
    )(token_blocks, key_weight, value_weight)


def attention_kernel(scale, query_ref, key_ref, value_ref, high_ref, total_ref, summed_ref, short_ref):
    scores = lax.dot_general(
        query_ref[...], key_ref[0], (((1,), (1,)), ((), ())), preferred_element_type=jnp.float32
    ) * scale
    high = jnp.max(scores, axis=-1, keepdims=True)
    expo = jnp.exp(scores - high)
    total = jnp.sum(expo, axis=-1, keepdims=True)
    rows = high.shape[0]
    high_ref[0] = jnp.transpose(jnp.broadcast_to(high, (rows, 128)))[0:1, :]
    total_ref[0] = jnp.transpose(jnp.broadcast_to(total, (rows, 128)))[0:1, :]
    summed = jnp.dot(expo.astype(jnp.bfloat16), value_ref[0], preferred_element_type=jnp.float32)
    summed_ref[0] = summed
    short_ref[0] = summed.astype(jnp.bfloat16)


def attention(query_blocks, key_rows, value_rows, first, stride):
    _, frames, rows, width = query_blocks.shape
    keys = key_rows.shape[1]
    picked = 2
    scale = 1.0 / math.sqrt(width)
    stat = jax.ShapeDtypeStruct((frames, 1, picked * rows), jnp.float32)
    stat_spec = pl.BlockSpec((1, 1, rows), lambda f, i: (f, 0, i))
    row_spec = pl.BlockSpec((1, rows, width), lambda f, i: (f, i, 0))
    key_spec = pl.BlockSpec((1, keys, width), lambda f, i: (f, 0, 0))
    return pl.pallas_call(
        functools.partial(attention_kernel, scale),
        grid=(frames, picked),
        in_specs=[
            pl.BlockSpec((None, None, rows, width), lambda f, i: (first + stride * i, f, 0, 0)),
            key_spec,
            key_spec,
        ],
        out_specs=[stat_spec, stat_spec, row_spec, row_spec],
        out_shape=[
            stat,
            stat,
            jax.ShapeDtypeStruct((frames, picked * rows, width), jnp.float32),
            jax.ShapeDtypeStruct((frames, picked * rows, width), jnp.bfloat16),
        ],
        cost_estimate=pl.CostEstimate(
            flops=4 * frames * picked * rows * keys * width,
            transcendentals=frames * picked * rows * keys,
            bytes_accessed=4 * frames * keys * width + 8 * frames * picked * rows * width,
        ),
    )(query_blocks, key_rows, value_rows)


def per_device(features, query_weight, key_weight, value_weight, out_weight, conv_weight):
    frames, rows, cols, width = features.shape
    count = rows * cols
    widened = features.astype(jnp.float32)
    normed = rms_rows(widened).astype(jnp.bfloat16)
    flat = normed.reshape(frames * count, width)
    scale = 1.0 / math.sqrt(width)

    query = project(flat, query_weight).reshape(frames, count, width)
    query_rel = ring_gather(query, "z")
    inner = jnp.stack(ring_gather(normed.reshape(frames, count, width), "y"))
    outer = jnp.stack(ring_gather(inner, "x", halve=True))
    token_blocks = outer.reshape(-1, *outer.shape[2:])
    query_blocks = jnp.stack(query_rel)
    key_rows, value_rows = project_keys(token_blocks, key_weight, value_weight)

    blocks = len(query_rel)
    right_first = blocks // 2
    left_first = (blocks + 1) // 2 + 1
    parts = [None] * blocks
    for step in range(blocks // 2):
        first, second = (right_first - step) % blocks, (left_first + step) % blocks
        if step == blocks // 2 - 1:
            second = 0
        high, total, summed, short = attention(query_blocks, key_rows, value_rows, first, second - first)
        for j, k in enumerate((first, second)):
            rows_of = short if step == 0 else summed
            piece = slice(j * count, (j + 1) * count)
            parts[k] = (high[:, 0, piece], total[:, 0, piece], rows_of[:, piece])
    _, total, summed = ring_reduce(parts, "z", count)
    attended = (summed / total[..., None]).astype(jnp.bfloat16)

    projected = jnp.dot(attended.reshape(-1, width), out_weight, preferred_element_type=jnp.float32)
    mixed = (widened + projected.reshape(features.shape)).astype(jnp.bfloat16)
    mixed_wide = mixed.astype(jnp.float32)
    activated = jax.nn.silu(rms_rows(mixed_wide)).astype(jnp.bfloat16)

    every = ("tm", *ROW_AXES)
    count_rows = 1
    for name in ROW_AXES:
        count_rows *= lax.axis_size(name)
    earlier = lax.ppermute(activated, "tm", [(0, 1)])
    earlier_above = lax.ppermute(activated, every, [(r, count_rows + r + 1) for r in range(count_rows - 1)])
    earlier_below = lax.ppermute(activated, every, [(r + 1, count_rows + r) for r in range(count_rows - 1)])
    above = jnp.concatenate([earlier_above, row_shift(activated, True)], axis=0)
    below = jnp.concatenate([earlier_below, row_shift(activated, False)], axis=0)
    stacked = jnp.concatenate([earlier, activated], axis=0)
    padded = jnp.concatenate([above, stacked, below], axis=1)
    padded = jnp.pad(padded, ((0, 0), (0, 0), (1, 1), (0, 0)))
    patches = []
    for tap_time in range(3):
        for tap_row in range(3):
            for tap_col in range(3):
                patches.append(
                    padded[
                        tap_time : tap_time + frames,
                        tap_row : tap_row + rows,
                        tap_col : tap_col + cols,
                    ]
                )
    columns = jnp.concatenate(patches, axis=-1).reshape(frames * count, 27 * width)
    conv = jnp.dot(
        columns, conv_weight.reshape(27 * width, width), preferred_element_type=jnp.float32
    )
    return (mixed_wide + conv.reshape(features.shape)).astype(jnp.bfloat16)


def solution(mesh):
    sizes = dict(zip(mesh.axis_names, mesh.devices.shape))
    tile = sizes["tile"]
    y = 4
    z = 8
    x = tile // (y * z)
    fine = Mesh(mesh.devices.reshape(sizes["tm"], x, z, y), ("tm", *ROW_AXES))
    spec = P("tm", ROW_AXES, None, None)
    in_specs = (spec, P(), P(), P(), P(), P())
    return jax.shard_map(
        per_device, mesh=fine, in_specs=in_specs, out_specs=spec, check_vma=False
    )
```

```python
import functools
import math

import jax
import jax.numpy as jnp
from jax import lax
from jax.experimental import pallas as pl
from jax.experimental.pallas import tpu as pltpu
from jax.sharding import Mesh
from jax.sharding import PartitionSpec as P

ROW_AXES = ("x", "z", "y")


def rms_rows(values):
    return values * lax.rsqrt(jnp.mean(values * values, axis=-1, keepdims=True) + 1e-06)


def project(flat_rows, weight):
    return jnp.dot(flat_rows, weight, preferred_element_type=jnp.float32).astype(jnp.bfloat16)


def ring_shift(block, axis, step):
    n = lax.axis_size(axis)
    return lax.ppermute(block, axis, [(i, (i + step) % n) for i in range(n)])


def ring_gather(block, axis, halve=False):
    n = lax.axis_size(axis)
    rel = [None] * n
    rel[0] = block
    right = left = block
    for s in range(1, n // 2):
        right = ring_shift(right, axis, 1)
        rel[n - s] = right
        left = ring_shift(left, axis, -1)
        rel[s] = left
    if halve:
        half = block.shape[0] // 2
        head = ring_shift(right[:half], axis, 1)
        tail = ring_shift(left[half:], axis, -1)
        rel[n // 2] = jnp.concatenate([head, tail], axis=0)
    else:
        rel[n // 2] = ring_shift(right, axis, 1)
    return rel


def split3(values):
    hi = values.astype(jnp.bfloat16)
    rest = values - hi.astype(jnp.float32)
    mid = rest.astype(jnp.bfloat16)
    lo = (rest - mid.astype(jnp.float32)).astype(jnp.bfloat16)
    return [hi, mid, lo]


def join3(parts):
    hi, mid, lo = (p.astype(jnp.float32) for p in parts)
    return (hi + mid) + lo


def pack(state):
    high, total, summed = state
    frames, rows, width = summed.shape
    stats = jnp.stack(split3(high) + split3(total), axis=1).reshape(frames, -1, width)
    return jnp.concatenate([summed.astype(jnp.bfloat16), stats], axis=1)


def unpack(payload, rows):
    frames, _, width = payload.shape
    summed = payload[:, :rows].astype(jnp.float32)
    stats = payload[:, rows:].reshape(frames, 6, rows)
    high = join3([stats[:, 0], stats[:, 1], stats[:, 2]])
    total = join3([stats[:, 3], stats[:, 4], stats[:, 5]])
    return high, total, summed


def combine(first, second):
    high_a, total_a, summed_a = first
    high_b, total_b, summed_b = second
    fresh = jnp.maximum(high_a, high_b)
    weight_a = jnp.exp(high_a - fresh)
    weight_b = jnp.exp(high_b - fresh)
    total = total_a * weight_a + total_b * weight_b
    summed = summed_a * weight_a[..., None] + summed_b * weight_b[..., None]
    return fresh, total, summed


def ring_reduce(parts, axis, rows):
    n = lax.axis_size(axis)
    right_hops = n // 2
    left_hops = n - 1 - right_hops
    right = parts[right_hops]
    for s in range(1, right_hops + 1):
        right = unpack(ring_shift(pack(right), axis, 1), rows)
        if s < right_hops:
            right = combine(right, parts[right_hops - s])
    left = parts[(n - left_hops) % n]
    for s in range(1, left_hops + 1):
        left = unpack(ring_shift(pack(left), axis, -1), rows)
        if s < left_hops:
            left = combine(left, parts[(n - left_hops + s) % n])
    return combine(combine(right, left), parts[0])


def row_shift(block, forward):
    count = 1
    for name in ROW_AXES:
        count *= lax.axis_size(name)
    if forward:
        route = [(i, i + 1) for i in range(count - 1)]
    else:
        route = [(i + 1, i) for i in range(count - 1)]
    return lax.ppermute(block, ROW_AXES, route)


def attention_kernel(
    scale, query_ref, token_ref, key_w_ref, value_w_ref,
    high_ref, total_ref, summed_ref, short_ref, key_scr, value_scr,
):
    width = key_scr.shape[-1]

    @pl.when(pl.program_id(1) == 0)
    def _():
        tokens = token_ref[...].reshape(-1, width)
        key_scr[...] = jnp.dot(tokens, key_w_ref[...], preferred_element_type=jnp.float32).astype(jnp.bfloat16)
        value_scr[...] = jnp.dot(tokens, value_w_ref[...], preferred_element_type=jnp.float32).astype(jnp.bfloat16)

    query = query_ref[...].reshape(-1, width)
    scores = lax.dot_general(
        query, key_scr[...], (((1,), (1,)), ((), ())), preferred_element_type=jnp.float32
    ) * scale
    high = jnp.max(scores, axis=-1, keepdims=True)
    expo = jnp.exp(scores - high)
    total = jnp.sum(expo, axis=-1, keepdims=True)
    rows = high.shape[0]
    high_ref[0] = jnp.transpose(jnp.broadcast_to(high, (rows, 128)))[0:1, :]
    total_ref[0] = jnp.transpose(jnp.broadcast_to(total, (rows, 128)))[0:1, :]
    summed = jnp.dot(expo.astype(jnp.bfloat16), value_scr[...], preferred_element_type=jnp.float32)
    summed_ref[0] = summed
    short_ref[0] = summed.astype(jnp.bfloat16)


def attention(query_blocks, token_blocks, key_weight, value_weight):
    query_count, frames, rows, width = query_blocks.shape
    key_count = token_blocks.shape[0]
    per_tile = 4
    tile = per_tile * rows
    queries = query_count * rows
    scale = 1.0 / math.sqrt(width)
    stat = jax.ShapeDtypeStruct((frames, 1, queries), jnp.float32)
    stat_spec = pl.BlockSpec((1, 1, tile), lambda f, i: (f, 0, i))
    row_spec = pl.BlockSpec((1, tile, width), lambda f, i: (f, i, 0))
    weight_spec = pl.BlockSpec((width, width), lambda f, i: (0, 0))
    keys = key_count * rows
    return pl.pallas_call(
        functools.partial(attention_kernel, scale),
        grid=(frames, query_count // per_tile),
        in_specs=[
            pl.BlockSpec((per_tile, None, rows, width), lambda f, i: (i, f, 0, 0)),
            pl.BlockSpec((key_count, None, rows, width), lambda f, i: (0, f, 0, 0)),
            weight_spec,
            weight_spec,
        ],
        out_specs=[stat_spec, stat_spec, row_spec, row_spec],
        out_shape=[
            stat,
            stat,
            jax.ShapeDtypeStruct((frames, queries, width), jnp.float32),
            jax.ShapeDtypeStruct((frames, queries, width), jnp.bfloat16),
        ],
        scratch_shapes=[
            pltpu.VMEM((keys, width), jnp.bfloat16),
            pltpu.VMEM((keys, width), jnp.bfloat16),
        ],
        cost_estimate=pl.CostEstimate(
            flops=4 * frames * queries * keys * width + 4 * frames * keys * width * width,
            transcendentals=frames * queries * keys,
            bytes_accessed=2 * frames * (queries + keys) * width + 6 * frames * queries * width,
        ),
    )(query_blocks, token_blocks, key_weight, value_weight)


def per_device(features, query_weight, key_weight, value_weight, out_weight, conv_weight):
    frames, rows, cols, width = features.shape
    count = rows * cols
    widened = features.astype(jnp.float32)
    normed = rms_rows(widened).astype(jnp.bfloat16)
    flat = normed.reshape(frames * count, width)
    scale = 1.0 / math.sqrt(width)

    query = project(flat, query_weight).reshape(frames, count, width)
    query_rel = ring_gather(query, "z")
    inner = jnp.stack(ring_gather(normed.reshape(frames, count, width), "y"))
    outer = jnp.stack(ring_gather(inner, "x", halve=True))
    token_blocks = outer.reshape(-1, *outer.shape[2:])
    query_blocks = jnp.stack(query_rel)
    highest, total, summed, short = attention(query_blocks, token_blocks, key_weight, value_weight)
    highest, total = highest[:, 0], total[:, 0]

    blocks = len(query_rel)
    first_sent = (blocks // 2, (blocks + 1) // 2 + 1)
    parts = []
    for k in range(blocks):
        lo, hi = k * count, (k + 1) * count
        rows_of = short if k in first_sent else summed
        parts.append((highest[:, lo:hi], total[:, lo:hi], rows_of[:, lo:hi]))
    _, total, summed = ring_reduce(parts, "z", count)
    attended = (summed / total[..., None]).astype(jnp.bfloat16)

    projected = jnp.dot(attended.reshape(-1, width), out_weight, preferred_element_type=jnp.float32)
    mixed = (widened + projected.reshape(features.shape)).astype(jnp.bfloat16)
    mixed_wide = mixed.astype(jnp.float32)
    activated = jax.nn.silu(rms_rows(mixed_wide)).astype(jnp.bfloat16)

    every = ("tm", *ROW_AXES)
    count_rows = 1
    for name in ROW_AXES:
        count_rows *= lax.axis_size(name)
    earlier = lax.ppermute(activated, "tm", [(0, 1)])
    earlier_above = lax.ppermute(activated, every, [(r, count_rows + r + 1) for r in range(count_rows - 1)])
    earlier_below = lax.ppermute(activated, every, [(r + 1, count_rows + r) for r in range(count_rows - 1)])
    above = jnp.concatenate([earlier_above, row_shift(activated, True)], axis=0)
    below = jnp.concatenate([earlier_below, row_shift(activated, False)], axis=0)
    stacked = jnp.concatenate([earlier, activated], axis=0)
    padded = jnp.concatenate([above, stacked, below], axis=1)
    padded = jnp.pad(padded, ((0, 0), (0, 0), (1, 1), (0, 0)))
    patches = []
    for tap_time in range(3):
        for tap_row in range(3):
            for tap_col in range(3):
                patches.append(
                    padded[
                        tap_time : tap_time + frames,
                        tap_row : tap_row + rows,
                        tap_col : tap_col + cols,
                    ]
                )
    columns = jnp.concatenate(patches, axis=-1).reshape(frames * count, 27 * width)
    conv = jnp.dot(
        columns, conv_weight.reshape(27 * width, width), preferred_element_type=jnp.float32
    )
    return (mixed_wide + conv.reshape(features.shape)).astype(jnp.bfloat16)


def solution(mesh):
    sizes = dict(zip(mesh.axis_names, mesh.devices.shape))
    tile = sizes["tile"]
    y = 4
    z = 8
    x = tile // (y * z)
    fine = Mesh(mesh.devices.reshape(sizes["tm"], x, z, y), ("tm", *ROW_AXES))
    spec = P("tm", ROW_AXES, None, None)
    in_specs = (spec, P(), P(), P(), P(), P())
    return jax.shard_map(
        per_device, mesh=fine, in_specs=in_specs, out_specs=spec, check_vma=False
    )
```

```python
import functools
import math

import jax
import jax.numpy as jnp
from jax import lax
from jax.experimental import pallas as pl
from jax.experimental.pallas import tpu as pltpu
from jax.sharding import Mesh
from jax.sharding import PartitionSpec as P

ROW_AXES = ("x", "z", "y")


def rms_rows(values):
    return values * lax.rsqrt(jnp.mean(values * values, axis=-1, keepdims=True) + 1e-06)


def project(flat_rows, weight):
    return jnp.dot(flat_rows, weight, preferred_element_type=jnp.float32).astype(jnp.bfloat16)


def ring_shift(block, axis, step):
    n = lax.axis_size(axis)
    return lax.ppermute(block, axis, [(i, (i + step) % n) for i in range(n)])


def ring_gather(block, axis, halve=False):
    n = lax.axis_size(axis)
    rel = [None] * n
    rel[0] = block
    right = left = block
    for s in range(1, n // 2):
        right = ring_shift(right, axis, 1)
        rel[n - s] = right
        left = ring_shift(left, axis, -1)
        rel[s] = left
    if halve:
        half = block.shape[0] // 2
        head = ring_shift(right[:half], axis, 1)
        tail = ring_shift(left[half:], axis, -1)
        rel[n // 2] = jnp.concatenate([head, tail], axis=0)
    else:
        rel[n // 2] = ring_shift(right, axis, 1)
    return rel


def split3(values):
    hi = values.astype(jnp.bfloat16)
    rest = values - hi.astype(jnp.float32)
    mid = rest.astype(jnp.bfloat16)
    lo = (rest - mid.astype(jnp.float32)).astype(jnp.bfloat16)
    return [hi, mid, lo]


def join3(parts):
    hi, mid, lo = (p.astype(jnp.float32) for p in parts)
    return (hi + mid) + lo


def pack(state):
    high, total, summed = state
    frames, rows, width = summed.shape
    stats = jnp.stack(split3(high) + split3(total), axis=1).reshape(frames, -1, width)
    return jnp.concatenate([summed.astype(jnp.bfloat16), stats], axis=1)


def unpack(payload, rows):
    frames, _, width = payload.shape
    summed = payload[:, :rows].astype(jnp.float32)
    stats = payload[:, rows:].reshape(frames, 6, rows)
    high = join3([stats[:, 0], stats[:, 1], stats[:, 2]])
    total = join3([stats[:, 3], stats[:, 4], stats[:, 5]])
    return high, total, summed


def combine(first, second):
    high_a, total_a, summed_a = first
    high_b, total_b, summed_b = second
    fresh = jnp.maximum(high_a, high_b)
    weight_a = jnp.exp(high_a - fresh)
    weight_b = jnp.exp(high_b - fresh)
    total = total_a * weight_a + total_b * weight_b
    summed = summed_a * weight_a[..., None] + summed_b * weight_b[..., None]
    return fresh, total, summed


def ring_reduce(parts, axis, rows):
    n = lax.axis_size(axis)
    right_hops = n // 2
    left_hops = n - 1 - right_hops
    right = parts[right_hops]
    for s in range(1, right_hops + 1):
        right = unpack(ring_shift(pack(right), axis, 1), rows)
        if s < right_hops:
            right = combine(right, parts[right_hops - s])
    left = parts[(n - left_hops) % n]
    for s in range(1, left_hops + 1):
        left = unpack(ring_shift(pack(left), axis, -1), rows)
        if s < left_hops:
            left = combine(left, parts[(n - left_hops + s) % n])
    return combine(combine(right, left), parts[0])


def row_shift(block, forward):
    count = 1
    for name in ROW_AXES:
        count *= lax.axis_size(name)
    if forward:
        route = [(i, i + 1) for i in range(count - 1)]
    else:
        route = [(i + 1, i) for i in range(count - 1)]
    return lax.ppermute(block, ROW_AXES, route)


def attention_kernel(
    scale, query_ref, first_ref, second_ref, key_w_ref, value_w_ref,
    high_ref, total_ref, summed_ref, short_ref, key_scr, value_scr,
):
    width = key_scr.shape[-1]
    half = key_scr.shape[0] // 2

    @pl.when(pl.program_id(1) == 0)
    def _():
        for lo, token_ref in ((0, first_ref), (half, second_ref)):
            tokens = token_ref[...].reshape(-1, width)
            key_scr[lo : lo + half] = jnp.dot(
                tokens, key_w_ref[...], preferred_element_type=jnp.float32
            ).astype(jnp.bfloat16)
            value_scr[lo : lo + half] = jnp.dot(
                tokens, value_w_ref[...], preferred_element_type=jnp.float32
            ).astype(jnp.bfloat16)

    query = query_ref[...].reshape(-1, width)
    scores = lax.dot_general(
        query, key_scr[...], (((1,), (1,)), ((), ())), preferred_element_type=jnp.float32
    ) * scale
    high = jnp.max(scores, axis=-1, keepdims=True)
    expo = jnp.exp(scores - high)
    total = jnp.sum(expo, axis=-1, keepdims=True)
    rows = high.shape[0]
    high_ref[0] = jnp.transpose(jnp.broadcast_to(high, (rows, 128)))[0:1, :]
    total_ref[0] = jnp.transpose(jnp.broadcast_to(total, (rows, 128)))[0:1, :]
    summed = jnp.dot(expo.astype(jnp.bfloat16), value_scr[...], preferred_element_type=jnp.float32)
    summed_ref[0] = summed
    short_ref[0] = summed.astype(jnp.bfloat16)


def attention(query_blocks, first_blocks, second_blocks, key_weight, value_weight):
    query_count, frames, rows, width = query_blocks.shape
    key_count = first_blocks.shape[0]
    per_tile = 4
    tile = per_tile * rows
    queries = query_count * rows
    scale = 1.0 / math.sqrt(width)
    stat = jax.ShapeDtypeStruct((frames, 1, queries), jnp.float32)
    stat_spec = pl.BlockSpec((1, 1, tile), lambda f, i: (f, 0, i))
    row_spec = pl.BlockSpec((1, tile, width), lambda f, i: (f, i, 0))
    weight_spec = pl.BlockSpec((width, width), lambda f, i: (0, 0))
    keys = key_count * rows
    return pl.pallas_call(
        functools.partial(attention_kernel, scale),
        grid=(frames, query_count // per_tile),
        in_specs=[
            pl.BlockSpec((per_tile, None, rows, width), lambda f, i: (i, f, 0, 0)),
            pl.BlockSpec((key_count, None, rows // 2, width), lambda f, i: (0, f, 0, 0)),
            pl.BlockSpec((key_count, None, rows // 2, width), lambda f, i: (0, f, 0, 0)),
            weight_spec,
            weight_spec,
        ],
        out_specs=[stat_spec, stat_spec, row_spec, row_spec],
        out_shape=[
            stat,
            stat,
            jax.ShapeDtypeStruct((frames, queries, width), jnp.float32),
            jax.ShapeDtypeStruct((frames, queries, width), jnp.bfloat16),
        ],
        scratch_shapes=[
            pltpu.VMEM((keys, width), jnp.bfloat16),
            pltpu.VMEM((keys, width), jnp.bfloat16),
        ],
        cost_estimate=pl.CostEstimate(
            flops=4 * frames * queries * keys * width + 4 * frames * keys * width * width,
            transcendentals=frames * queries * keys,
            bytes_accessed=2 * frames * (queries + keys) * width + 6 * frames * queries * width,
        ),
    )(query_blocks, first_blocks, second_blocks, key_weight, value_weight)


def per_device(features, query_weight, key_weight, value_weight, out_weight, conv_weight):
    frames, rows, cols, width = features.shape
    count = rows * cols
    widened = features.astype(jnp.float32)
    normed = rms_rows(widened).astype(jnp.bfloat16)
    flat = normed.reshape(frames * count, width)
    scale = 1.0 / math.sqrt(width)

    query = project(flat, query_weight).reshape(frames, count, width)
    query_rel = ring_gather(query, "z")
    tokens = normed.reshape(frames, count, width)
    half = count // 2
    chains = []
    for part, (first, second) in ((tokens[:, :half], ("y", "x")), (tokens[:, half:], ("x", "y"))):
        inner = jnp.stack(ring_gather(part, first))
        outer = jnp.stack(ring_gather(inner, second, halve=True))
        chains.append(outer.reshape(-1, *outer.shape[2:]))
    query_blocks = jnp.stack(query_rel)
    highest, total, summed, short = attention(query_blocks, chains[0], chains[1], key_weight, value_weight)
    highest, total = highest[:, 0], total[:, 0]

    blocks = len(query_rel)
    first_sent = (blocks // 2, (blocks + 1) // 2 + 1)
    parts = []
    for k in range(blocks):
        lo, hi = k * count, (k + 1) * count
        rows_of = short if k in first_sent else summed
        parts.append((highest[:, lo:hi], total[:, lo:hi], rows_of[:, lo:hi]))
    _, total, summed = ring_reduce(parts, "z", count)
    attended = (summed / total[..., None]).astype(jnp.bfloat16)

    projected = jnp.dot(attended.reshape(-1, width), out_weight, preferred_element_type=jnp.float32)
    mixed = (widened + projected.reshape(features.shape)).astype(jnp.bfloat16)
    mixed_wide = mixed.astype(jnp.float32)
    activated = jax.nn.silu(rms_rows(mixed_wide)).astype(jnp.bfloat16)

    every = ("tm", *ROW_AXES)
    count_rows = 1
    for name in ROW_AXES:
        count_rows *= lax.axis_size(name)
    earlier = lax.ppermute(activated, "tm", [(0, 1)])
    earlier_above = lax.ppermute(activated, every, [(r, count_rows + r + 1) for r in range(count_rows - 1)])
    earlier_below = lax.ppermute(activated, every, [(r + 1, count_rows + r) for r in range(count_rows - 1)])
    above = jnp.concatenate([earlier_above, row_shift(activated, True)], axis=0)
    below = jnp.concatenate([earlier_below, row_shift(activated, False)], axis=0)
    stacked = jnp.concatenate([earlier, activated], axis=0)
    padded = jnp.concatenate([above, stacked, below], axis=1)
    padded = jnp.pad(padded, ((0, 0), (0, 0), (1, 1), (0, 0)))
    patches = []
    for tap_time in range(3):
        for tap_row in range(3):
            for tap_col in range(3):
                patches.append(
                    padded[
                        tap_time : tap_time + frames,
                        tap_row : tap_row + rows,
                        tap_col : tap_col + cols,
                    ]
                )
    columns = jnp.concatenate(patches, axis=-1).reshape(frames * count, 27 * width)
    conv = jnp.dot(
        columns, conv_weight.reshape(27 * width, width), preferred_element_type=jnp.float32
    )
    return (mixed_wide + conv.reshape(features.shape)).astype(jnp.bfloat16)


def solution(mesh):
    sizes = dict(zip(mesh.axis_names, mesh.devices.shape))
    tile = sizes["tile"]
    y = 4
    z = 8
    x = tile // (y * z)
    fine = Mesh(mesh.devices.reshape(sizes["tm"], x, z, y), ("tm", *ROW_AXES))
    spec = P("tm", ROW_AXES, None, None)
    in_specs = (spec, P(), P(), P(), P(), P())
    return jax.shard_map(
        per_device, mesh=fine, in_specs=in_specs, out_specs=spec, check_vma=False
    )
```

```python
import functools
import math

import jax
import jax.numpy as jnp
from jax import lax
from jax.experimental import pallas as pl
from jax.experimental.pallas import tpu as pltpu
from jax.sharding import Mesh
from jax.sharding import PartitionSpec as P

ROW_AXES = ("x", "z", "y")


def rms_rows(values):
    return values * lax.rsqrt(jnp.mean(values * values, axis=-1, keepdims=True) + 1e-06)


def project(flat_rows, weight):
    return jnp.dot(flat_rows, weight, preferred_element_type=jnp.float32).astype(jnp.bfloat16)


def ring_shift(block, axis, step):
    n = lax.axis_size(axis)
    return lax.ppermute(block, axis, [(i, (i + step) % n) for i in range(n)])


def ring_gather(block, axis, halve=False):
    n = lax.axis_size(axis)
    rel = [None] * n
    rel[0] = block
    right = left = block
    for s in range(1, n // 2):
        right = ring_shift(right, axis, 1)
        rel[n - s] = right
        left = ring_shift(left, axis, -1)
        rel[s] = left
    if halve:
        half = block.shape[0] // 2
        head = ring_shift(right[:half], axis, 1)
        tail = ring_shift(left[half:], axis, -1)
        rel[n // 2] = jnp.concatenate([head, tail], axis=0)
    else:
        rel[n // 2] = ring_shift(right, axis, 1)
    return rel


def split3(values):
    hi = values.astype(jnp.bfloat16)
    rest = values - hi.astype(jnp.float32)
    mid = rest.astype(jnp.bfloat16)
    lo = (rest - mid.astype(jnp.float32)).astype(jnp.bfloat16)
    return [hi, mid, lo]


def join3(parts):
    hi, mid, lo = (p.astype(jnp.float32) for p in parts)
    return (hi + mid) + lo


def pack(state):
    high, total, summed = state
    frames, rows, width = summed.shape
    stats = jnp.stack(split3(high) + split3(total), axis=1).reshape(frames, -1, width)
    return jnp.concatenate([summed.astype(jnp.bfloat16), stats], axis=1)


def unpack(payload, rows):
    frames, _, width = payload.shape
    summed = payload[:, :rows].astype(jnp.float32)
    stats = payload[:, rows:].reshape(frames, 6, rows)
    high = join3([stats[:, 0], stats[:, 1], stats[:, 2]])
    total = join3([stats[:, 3], stats[:, 4], stats[:, 5]])
    return high, total, summed


def combine(first, second):
    high_a, total_a, summed_a = first
    high_b, total_b, summed_b = second
    fresh = jnp.maximum(high_a, high_b)
    weight_a = jnp.exp(high_a - fresh)
    weight_b = jnp.exp(high_b - fresh)
    total = total_a * weight_a + total_b * weight_b
    summed = summed_a * weight_a[..., None] + summed_b * weight_b[..., None]
    return fresh, total, summed


def ring_reduce(parts, axis, rows):
    n = lax.axis_size(axis)
    right_hops = n // 2
    left_hops = n - 1 - right_hops
    right = parts[right_hops]
    for s in range(1, right_hops + 1):
        right = unpack(ring_shift(pack(right), axis, 1), rows)
        if s < right_hops:
            right = combine(right, parts[right_hops - s])
    left = parts[(n - left_hops) % n]
    for s in range(1, left_hops + 1):
        left = unpack(ring_shift(pack(left), axis, -1), rows)
        if s < left_hops:
            left = combine(left, parts[(n - left_hops + s) % n])
    return combine(combine(right, left), parts[0])


def row_shift(block, forward):
    count = 1
    for name in ROW_AXES:
        count *= lax.axis_size(name)
    if forward:
        route = [(i, i + 1) for i in range(count - 1)]
    else:
        route = [(i + 1, i) for i in range(count - 1)]
    return lax.ppermute(block, ROW_AXES, route)


def attention_kernel(
    scale, query_ref, first_ref, second_ref, key_w_ref, value_w_ref,
    high_ref, total_ref, summed_ref, short_ref, key_scr, value_scr,
):
    width = key_scr.shape[-1]
    half = key_scr.shape[0] // 2

    @pl.when(pl.program_id(1) == 0)
    def _():
        for lo, token_ref in ((0, first_ref), (half, second_ref)):
            tokens = token_ref[...].reshape(-1, width)
            key_scr[lo : lo + half] = jnp.dot(
                tokens, key_w_ref[...], preferred_element_type=jnp.float32
            ).astype(jnp.bfloat16)
            value_scr[lo : lo + half] = jnp.dot(
                tokens, value_w_ref[...], preferred_element_type=jnp.float32
            ).astype(jnp.bfloat16)

    query = query_ref[...].reshape(-1, width)
    scores = lax.dot_general(
        query, key_scr[...], (((1,), (1,)), ((), ())), preferred_element_type=jnp.float32
    ) * scale
    high = jnp.max(scores, axis=-1, keepdims=True)
    expo = jnp.exp(scores - high)
    total = jnp.sum(expo, axis=-1, keepdims=True)
    rows = high.shape[0]
    high_ref[0] = jnp.transpose(jnp.broadcast_to(high, (rows, 128)))[0:1, :]
    total_ref[0] = jnp.transpose(jnp.broadcast_to(total, (rows, 128)))[0:1, :]
    summed = jnp.dot(expo.astype(jnp.bfloat16), value_scr[...], preferred_element_type=jnp.float32)
    summed_ref[0] = summed
    short_ref[0] = summed.astype(jnp.bfloat16)


def attention(query_blocks, first_blocks, second_blocks, key_weight, value_weight):
    query_count, frames, rows, width = query_blocks.shape
    key_count = first_blocks.shape[0]
    per_tile = 4
    tile = per_tile * rows
    queries = query_count * rows
    scale = 1.0 / math.sqrt(width)
    stat = jax.ShapeDtypeStruct((frames, 1, queries), jnp.float32)
    stat_spec = pl.BlockSpec((1, 1, tile), lambda f, i: (f, 0, i))
    row_spec = pl.BlockSpec((1, tile, width), lambda f, i: (f, i, 0))
    weight_spec = pl.BlockSpec((width, width), lambda f, i: (0, 0))
    keys = key_count * rows
    return pl.pallas_call(
        functools.partial(attention_kernel, scale),
        grid=(frames, query_count // per_tile),
        in_specs=[
            pl.BlockSpec((per_tile, None, rows, width), lambda f, i: (i, f, 0, 0)),
            pl.BlockSpec((key_count, None, rows // 2, width), lambda f, i: (0, f, 0, 0)),
            pl.BlockSpec((key_count, None, rows // 2, width), lambda f, i: (0, f, 0, 0)),
            weight_spec,
            weight_spec,
        ],
        out_specs=[stat_spec, stat_spec, row_spec, row_spec],
        out_shape=[
            stat,
            stat,
            jax.ShapeDtypeStruct((frames, queries, width), jnp.float32),
            jax.ShapeDtypeStruct((frames, queries, width), jnp.bfloat16),
        ],
        scratch_shapes=[
            pltpu.VMEM((keys, width), jnp.bfloat16),
            pltpu.VMEM((keys, width), jnp.bfloat16),
        ],
        cost_estimate=pl.CostEstimate(
            flops=4 * frames * queries * keys * width + 4 * frames * keys * width * width,
            transcendentals=frames * queries * keys,
            bytes_accessed=2 * frames * (queries + keys) * width + 6 * frames * queries * width,
        ),
    )(query_blocks, first_blocks, second_blocks, key_weight, value_weight)


def per_device(features, query_weight, key_weight, value_weight, out_weight, conv_weight):
    frames, rows, cols, width = features.shape
    count = rows * cols
    widened = features.astype(jnp.float32)
    normed = rms_rows(widened).astype(jnp.bfloat16)
    flat = normed.reshape(frames * count, width)
    scale = 1.0 / math.sqrt(width)

    query = project(flat, query_weight).reshape(frames, count, width)
    query_rel = ring_gather(query, "z")
    tokens = normed.reshape(frames, count, width)
    half = count // 2
    chains = []
    for part, (first, second) in ((tokens[:, :half], ("y", "x")), (tokens[:, half:], ("x", "y"))):
        inner = jnp.stack(ring_gather(part, first))
        outer = jnp.stack(ring_gather(inner, second, halve=True))
        chains.append(outer.reshape(-1, *outer.shape[2:]))
    query_blocks = jnp.stack(query_rel)
    highest, total, summed, short = attention(query_blocks, chains[0], chains[1], key_weight, value_weight)
    highest, total = highest[:, 0], total[:, 0]

    blocks = len(query_rel)
    first_sent = (blocks // 2, (blocks + 1) // 2 + 1)
    parts = []
    for k in range(blocks):
        lo, hi = k * count, (k + 1) * count
        rows_of = short if k in first_sent else summed
        parts.append((highest[:, lo:hi], total[:, lo:hi], rows_of[:, lo:hi]))
    _, total, summed = ring_reduce(parts, "z", count)
    attended = (summed / total[..., None]).astype(jnp.bfloat16)

    projected = jnp.dot(attended.reshape(-1, width), out_weight, preferred_element_type=jnp.float32)
    mixed = (widened + projected.reshape(features.shape)).astype(jnp.bfloat16)
    mixed_wide = mixed.astype(jnp.float32)
    activated = jax.nn.silu(rms_rows(mixed_wide)).astype(jnp.bfloat16)

    every = ("tm", *ROW_AXES)
    count_rows = 1
    for name in ROW_AXES:
        count_rows *= lax.axis_size(name)
    earlier = lax.ppermute(activated, "tm", [(0, 1)])
    earlier_above = lax.ppermute(activated, every, [(r, count_rows + r + 1) for r in range(count_rows - 1)])
    earlier_below = lax.ppermute(activated, every, [(r + 1, count_rows + r) for r in range(count_rows - 1)])
    above = jnp.concatenate([earlier_above, row_shift(activated, True)], axis=0)
    below = jnp.concatenate([earlier_below, row_shift(activated, False)], axis=0)
    stacked = jnp.concatenate([earlier, activated], axis=0)
    padded = jnp.concatenate([above, stacked, below], axis=1)
    padded = jnp.pad(padded, ((0, 0), (0, 0), (1, 1), (0, 0)))
    conv = lax.conv_general_dilated(
        padded[None],
        conv_weight,
        window_strides=(1, 1, 1),
        padding="VALID",
        dimension_numbers=("NDHWC", "DHWIO", "NDHWC"),
        preferred_element_type=jnp.float32,
    )
    return (mixed_wide + conv.reshape(features.shape)).astype(jnp.bfloat16)


def solution(mesh):
    sizes = dict(zip(mesh.axis_names, mesh.devices.shape))
    tile = sizes["tile"]
    y = 4
    z = 8
    x = tile // (y * z)
    fine = Mesh(mesh.devices.reshape(sizes["tm"], x, z, y), ("tm", *ROW_AXES))
    spec = P("tm", ROW_AXES, None, None)
    in_specs = (spec, P(), P(), P(), P(), P())
    return jax.shard_map(
        per_device, mesh=fine, in_specs=in_specs, out_specs=spec, check_vma=False
    )
```

```python
import functools
import math

import jax
import jax.numpy as jnp
from jax import lax
from jax.experimental import pallas as pl
from jax.experimental.pallas import tpu as pltpu
from jax.sharding import Mesh
from jax.sharding import PartitionSpec as P

ROW_AXES = ("x", "z", "y")


def rms_rows(values):
    return values * lax.rsqrt(jnp.mean(values * values, axis=-1, keepdims=True) + 1e-06)


def project(flat_rows, weight):
    return jnp.dot(flat_rows, weight, preferred_element_type=jnp.float32).astype(jnp.bfloat16)


def ring_shift(block, axis, step):
    n = lax.axis_size(axis)
    return lax.ppermute(block, axis, [(i, (i + step) % n) for i in range(n)])


def ring_gather(block, axis, halve=False):
    n = lax.axis_size(axis)
    rel = [None] * n
    rel[0] = block
    right = left = block
    for s in range(1, n // 2):
        right = ring_shift(right, axis, 1)
        rel[n - s] = right
        left = ring_shift(left, axis, -1)
        rel[s] = left
    if halve:
        half = block.shape[0] // 2
        head = ring_shift(right[:half], axis, 1)
        tail = ring_shift(left[half:], axis, -1)
        rel[n // 2] = jnp.concatenate([head, tail], axis=0)
    else:
        rel[n // 2] = ring_shift(right, axis, 1)
    return rel


def split3(values):
    hi = values.astype(jnp.bfloat16)
    rest = values - hi.astype(jnp.float32)
    mid = rest.astype(jnp.bfloat16)
    lo = (rest - mid.astype(jnp.float32)).astype(jnp.bfloat16)
    return [hi, mid, lo]


def join3(parts):
    hi, mid, lo = (p.astype(jnp.float32) for p in parts)
    return (hi + mid) + lo


def pack(state):
    high, total, summed = state
    frames, rows, width = summed.shape
    stats = jnp.stack(split3(high) + split3(total), axis=1).reshape(frames, -1, width)
    return jnp.concatenate([summed.astype(jnp.bfloat16), stats], axis=1)


def unpack(payload, rows):
    frames, _, width = payload.shape
    summed = payload[:, :rows].astype(jnp.float32)
    stats = payload[:, rows:].reshape(frames, 6, rows)
    high = join3([stats[:, 0], stats[:, 1], stats[:, 2]])
    total = join3([stats[:, 3], stats[:, 4], stats[:, 5]])
    return high, total, summed


def combine(first, second):
    high_a, total_a, summed_a = first
    high_b, total_b, summed_b = second
    fresh = jnp.maximum(high_a, high_b)
    weight_a = jnp.exp(high_a - fresh)
    weight_b = jnp.exp(high_b - fresh)
    total = total_a * weight_a + total_b * weight_b
    summed = summed_a * weight_a[..., None] + summed_b * weight_b[..., None]
    return fresh, total, summed


def ring_reduce(parts, axis, rows):
    n = lax.axis_size(axis)
    right_hops = n // 2
    left_hops = n - 1 - right_hops
    right = parts[right_hops]
    for s in range(1, right_hops + 1):
        right = unpack(ring_shift(pack(right), axis, 1), rows)
        if s < right_hops:
            right = combine(right, parts[right_hops - s])
    left = parts[(n - left_hops) % n]
    for s in range(1, left_hops + 1):
        left = unpack(ring_shift(pack(left), axis, -1), rows)
        if s < left_hops:
            left = combine(left, parts[(n - left_hops + s) % n])
    return combine(right, combine(left, parts[0]))


def row_shift(block, forward):
    count = 1
    for name in ROW_AXES:
        count *= lax.axis_size(name)
    if forward:
        route = [(i, i + 1) for i in range(count - 1)]
    else:
        route = [(i + 1, i) for i in range(count - 1)]
    return lax.ppermute(block, ROW_AXES, route)


def attention_kernel(
    scale, query_ref, first_ref, second_ref, key_w_ref, value_w_ref,
    high_ref, total_ref, summed_ref, short_ref, key_scr, value_scr,
):
    width = key_scr.shape[-1]
    half = key_scr.shape[0] // 2

    @pl.when(pl.program_id(1) == 0)
    def _():
        for lo, token_ref in ((0, first_ref), (half, second_ref)):
            tokens = token_ref[...].reshape(-1, width)
            key_scr[lo : lo + half] = jnp.dot(
                tokens, key_w_ref[...], preferred_element_type=jnp.float32
            ).astype(jnp.bfloat16)
            value_scr[lo : lo + half] = jnp.dot(
                tokens, value_w_ref[...], preferred_element_type=jnp.float32
            ).astype(jnp.bfloat16)

    query = query_ref[...].reshape(-1, width)
    scores = lax.dot_general(
        query, key_scr[...], (((1,), (1,)), ((), ())), preferred_element_type=jnp.float32
    ) * scale
    high = jnp.max(scores, axis=-1, keepdims=True)
    expo = jnp.exp(scores - high)
    total = jnp.sum(expo, axis=-1, keepdims=True)
    rows = high.shape[0]
    high_ref[0] = jnp.transpose(jnp.broadcast_to(high, (rows, 128)))[0:1, :]
    total_ref[0] = jnp.transpose(jnp.broadcast_to(total, (rows, 128)))[0:1, :]
    summed = jnp.dot(expo.astype(jnp.bfloat16), value_scr[...], preferred_element_type=jnp.float32)
    summed_ref[0] = summed
    short_ref[0] = summed.astype(jnp.bfloat16)


def attention(query_blocks, first_blocks, second_blocks, key_weight, value_weight):
    query_count, frames, rows, width = query_blocks.shape
    key_count = first_blocks.shape[0]
    per_tile = 4
    tile = per_tile * rows
    queries = query_count * rows
    scale = 1.0 / math.sqrt(width)
    stat = jax.ShapeDtypeStruct((frames, 1, queries), jnp.float32)
    stat_spec = pl.BlockSpec((1, 1, tile), lambda f, i: (f, 0, i))
    row_spec = pl.BlockSpec((1, tile, width), lambda f, i: (f, i, 0))
    weight_spec = pl.BlockSpec((width, width), lambda f, i: (0, 0))
    keys = key_count * rows
    return pl.pallas_call(
        functools.partial(attention_kernel, scale),
        grid=(frames, query_count // per_tile),
        in_specs=[
            pl.BlockSpec((per_tile, None, rows, width), lambda f, i: (i, f, 0, 0)),
            pl.BlockSpec((key_count, None, rows // 2, width), lambda f, i: (0, f, 0, 0)),
            pl.BlockSpec((key_count, None, rows // 2, width), lambda f, i: (0, f, 0, 0)),
            weight_spec,
            weight_spec,
        ],
        out_specs=[stat_spec, stat_spec, row_spec, row_spec],
        out_shape=[
            stat,
            stat,
            jax.ShapeDtypeStruct((frames, queries, width), jnp.float32),
            jax.ShapeDtypeStruct((frames, queries, width), jnp.bfloat16),
        ],
        scratch_shapes=[
            pltpu.VMEM((keys, width), jnp.bfloat16),
            pltpu.VMEM((keys, width), jnp.bfloat16),
        ],
        cost_estimate=pl.CostEstimate(
            flops=4 * frames * queries * keys * width + 4 * frames * keys * width * width,
            transcendentals=frames * queries * keys,
            bytes_accessed=2 * frames * (queries + keys) * width + 6 * frames * queries * width,
        ),
    )(query_blocks, first_blocks, second_blocks, key_weight, value_weight)


def per_device(features, query_weight, key_weight, value_weight, out_weight, conv_weight):
    frames, rows, cols, width = features.shape
    count = rows * cols
    widened = features.astype(jnp.float32)
    normed = rms_rows(widened).astype(jnp.bfloat16)
    flat = normed.reshape(frames * count, width)
    scale = 1.0 / math.sqrt(width)

    query = project(flat, query_weight).reshape(frames, count, width)
    query_rel = ring_gather(query, "z")
    tokens = normed.reshape(frames, count, width)
    half = count // 2
    chains = []
    for part, (first, second) in ((tokens[:, :half], ("y", "x")), (tokens[:, half:], ("x", "y"))):
        inner = jnp.stack(ring_gather(part, first))
        outer = jnp.stack(ring_gather(inner, second, halve=True))
        chains.append(outer.reshape(-1, *outer.shape[2:]))
    query_blocks = jnp.stack(query_rel)
    highest, total, summed, short = attention(query_blocks, chains[0], chains[1], key_weight, value_weight)
    highest, total = highest[:, 0], total[:, 0]

    blocks = len(query_rel)
    first_sent = (blocks // 2, (blocks + 1) // 2 + 1)
    parts = []
    for k in range(blocks):
        lo, hi = k * count, (k + 1) * count
        rows_of = short if k in first_sent else summed
        parts.append((highest[:, lo:hi], total[:, lo:hi], rows_of[:, lo:hi]))
    _, total, summed = ring_reduce(parts, "z", count)
    attended = (summed / total[..., None]).astype(jnp.bfloat16)

    projected = jnp.dot(attended.reshape(-1, width), out_weight, preferred_element_type=jnp.float32)
    mixed = (widened + projected.reshape(features.shape)).astype(jnp.bfloat16)
    mixed_wide = mixed.astype(jnp.float32)
    activated = jax.nn.silu(rms_rows(mixed_wide)).astype(jnp.bfloat16)

    every = ("tm", *ROW_AXES)
    count_rows = 1
    for name in ROW_AXES:
        count_rows *= lax.axis_size(name)
    earlier = lax.ppermute(activated, "tm", [(0, 1)])
    earlier_above = lax.ppermute(activated, every, [(r, count_rows + r + 1) for r in range(count_rows - 1)])
    earlier_below = lax.ppermute(activated, every, [(r + 1, count_rows + r) for r in range(count_rows - 1)])
    above = jnp.concatenate([earlier_above, row_shift(activated, True)], axis=0)
    below = jnp.concatenate([earlier_below, row_shift(activated, False)], axis=0)
    stacked = jnp.concatenate([earlier, activated], axis=0)
    padded = jnp.concatenate([above, stacked, below], axis=1)
    padded = jnp.pad(padded, ((0, 0), (0, 0), (1, 1), (0, 0)))
    patches = []
    for tap_time in range(3):
        for tap_row in range(3):
            for tap_col in range(3):
                patches.append(
                    padded[
                        tap_time : tap_time + frames,
                        tap_row : tap_row + rows,
                        tap_col : tap_col + cols,
                    ]
                )
    columns = jnp.concatenate(patches, axis=-1).reshape(frames * count, 27 * width)
    conv = jnp.dot(
        columns, conv_weight.reshape(27 * width, width), preferred_element_type=jnp.float32
    )
    return (mixed_wide + conv.reshape(features.shape)).astype(jnp.bfloat16)


def solution(mesh):
    sizes = dict(zip(mesh.axis_names, mesh.devices.shape))
    tile = sizes["tile"]
    y = 4
    z = 8
    x = tile // (y * z)
    fine = Mesh(mesh.devices.reshape(sizes["tm"], x, z, y), ("tm", *ROW_AXES))
    spec = P("tm", ROW_AXES, None, None)
    in_specs = (spec, P(), P(), P(), P(), P())
    return jax.shard_map(
        per_device, mesh=fine, in_specs=in_specs, out_specs=spec, check_vma=False
    )
```

```python
import functools
import math

import jax
import jax.numpy as jnp
from jax import lax
from jax.experimental import pallas as pl
from jax.experimental.pallas import tpu as pltpu
from jax.sharding import Mesh
from jax.sharding import PartitionSpec as P

ROW_AXES = ("x", "z", "y")


def rms_rows(values):
    return values * lax.rsqrt(jnp.mean(values * values, axis=-1, keepdims=True) + 1e-06)


def project(flat_rows, weight):
    return jnp.dot(flat_rows, weight, preferred_element_type=jnp.float32).astype(jnp.bfloat16)


def ring_shift(block, axis, step):
    n = lax.axis_size(axis)
    return lax.ppermute(block, axis, [(i, (i + step) % n) for i in range(n)])


def ring_gather(block, axis, halve=False):
    n = lax.axis_size(axis)
    rel = [None] * n
    rel[0] = block
    right = left = block
    for s in range(1, n // 2):
        right = ring_shift(right, axis, 1)
        rel[n - s] = right
        left = ring_shift(left, axis, -1)
        rel[s] = left
    if halve:
        half = block.shape[0] // 2
        head = ring_shift(right[:half], axis, 1)
        tail = ring_shift(left[half:], axis, -1)
        rel[n // 2] = jnp.concatenate([head, tail], axis=0)
    else:
        rel[n // 2] = ring_shift(right, axis, 1)
    return rel


def split3(values):
    hi = values.astype(jnp.bfloat16)
    rest = values - hi.astype(jnp.float32)
    mid = rest.astype(jnp.bfloat16)
    lo = (rest - mid.astype(jnp.float32)).astype(jnp.bfloat16)
    return [hi, mid, lo]


def join3(parts):
    hi, mid, lo = (p.astype(jnp.float32) for p in parts)
    return (hi + mid) + lo


def pack(state):
    high, total, summed = state
    frames, rows, width = summed.shape
    stats = jnp.stack(split3(high) + split3(total), axis=1).reshape(frames, -1, width)
    return jnp.concatenate([summed.astype(jnp.bfloat16), stats], axis=1)


def unpack(payload, rows):
    frames, _, width = payload.shape
    summed = payload[:, :rows].astype(jnp.float32)
    stats = payload[:, rows:].reshape(frames, 6, rows)
    high = join3([stats[:, 0], stats[:, 1], stats[:, 2]])
    total = join3([stats[:, 3], stats[:, 4], stats[:, 5]])
    return high, total, summed


def combine(first, second):
    high_a, total_a, summed_a = first
    high_b, total_b, summed_b = second
    fresh = jnp.maximum(high_a, high_b)
    weight_a = jnp.exp(high_a - fresh)
    weight_b = jnp.exp(high_b - fresh)
    total = total_a * weight_a + total_b * weight_b
    summed = summed_a * weight_a[..., None] + summed_b * weight_b[..., None]
    return fresh, total, summed


def ring_reduce(parts, axis, rows):
    n = lax.axis_size(axis)
    right_hops = n // 2
    left_hops = n - 1 - right_hops
    right = parts[right_hops]
    for s in range(1, right_hops + 1):
        right = unpack(ring_shift(pack(right), axis, 1), rows)
        if s < right_hops:
            right = combine(right, parts[right_hops - s])
    left = parts[(n - left_hops) % n]
    for s in range(1, left_hops + 1):
        left = unpack(ring_shift(pack(left), axis, -1), rows)
        if s < left_hops:
            left = combine(left, parts[(n - left_hops + s) % n])
    return combine(right, combine(left, parts[0]))


def row_shift(block, forward):
    count = 1
    for name in ROW_AXES:
        count *= lax.axis_size(name)
    if forward:
        route = [(i, i + 1) for i in range(count - 1)]
    else:
        route = [(i + 1, i) for i in range(count - 1)]
    return lax.ppermute(block, ROW_AXES, route)


def attention_kernel(
    scale, query_ref, first_ref, second_ref, key_w_ref, value_w_ref,
    high_ref, total_ref, summed_ref, short_ref, key_scr, value_scr,
):
    width = key_scr.shape[-1]
    half = key_scr.shape[0] // 2

    @pl.when(pl.program_id(1) == 0)
    def _():
        for lo, token_ref in ((0, first_ref), (half, second_ref)):
            tokens = token_ref[...].reshape(-1, width)
            key_scr[lo : lo + half] = jnp.dot(
                tokens, key_w_ref[...], preferred_element_type=jnp.float32
            ).astype(jnp.bfloat16)
            value_scr[lo : lo + half] = jnp.dot(
                tokens, value_w_ref[...], preferred_element_type=jnp.float32
            ).astype(jnp.bfloat16)

    query = query_ref[...].reshape(-1, width)
    scores = lax.dot_general(
        query, key_scr[...], (((1,), (1,)), ((), ())), preferred_element_type=jnp.float32
    ) * scale
    high = jnp.max(scores, axis=-1, keepdims=True)
    expo = jnp.exp(scores - high)
    total = jnp.sum(expo, axis=-1, keepdims=True)
    rows = high.shape[0]
    high_ref[0] = jnp.transpose(jnp.broadcast_to(high, (rows, 128)))[0:1, :]
    total_ref[0] = jnp.transpose(jnp.broadcast_to(total, (rows, 128)))[0:1, :]
    summed = jnp.dot(expo.astype(jnp.bfloat16), value_scr[...], preferred_element_type=jnp.float32)
    summed_ref[0] = summed
    short_ref[0] = summed.astype(jnp.bfloat16)


def attention(query_blocks, first_blocks, second_blocks, key_weight, value_weight):
    query_count, frames, rows, width = query_blocks.shape
    key_count = first_blocks.shape[0]
    per_tile = 4
    tile = per_tile * rows
    queries = query_count * rows
    scale = 1.0 / math.sqrt(width)
    stat = jax.ShapeDtypeStruct((frames, 1, queries), jnp.float32)
    stat_spec = pl.BlockSpec((1, 1, tile), lambda f, i: (f, 0, i))
    row_spec = pl.BlockSpec((1, tile, width), lambda f, i: (f, i, 0))
    weight_spec = pl.BlockSpec((width, width), lambda f, i: (0, 0))
    keys = key_count * rows
    return pl.pallas_call(
        functools.partial(attention_kernel, scale),
        grid=(frames, query_count // per_tile),
        in_specs=[
            pl.BlockSpec((per_tile, None, rows, width), lambda f, i: (i, f, 0, 0)),
            pl.BlockSpec((key_count, None, rows // 2, width), lambda f, i: (0, f, 0, 0)),
            pl.BlockSpec((key_count, None, rows // 2, width), lambda f, i: (0, f, 0, 0)),
            weight_spec,
            weight_spec,
        ],
        out_specs=[stat_spec, stat_spec, row_spec, row_spec],
        out_shape=[
            stat,
            stat,
            jax.ShapeDtypeStruct((frames, queries, width), jnp.float32),
            jax.ShapeDtypeStruct((frames, queries, width), jnp.bfloat16),
        ],
        scratch_shapes=[
            pltpu.VMEM((keys, width), jnp.bfloat16),
            pltpu.VMEM((keys, width), jnp.bfloat16),
        ],
        cost_estimate=pl.CostEstimate(
            flops=4 * frames * queries * keys * width + 4 * frames * keys * width * width,
            transcendentals=frames * queries * keys,
            bytes_accessed=2 * frames * (queries + keys) * width + 6 * frames * queries * width,
        ),
    )(query_blocks, first_blocks, second_blocks, key_weight, value_weight)


def per_device(features, query_weight, key_weight, value_weight, out_weight, conv_weight):
    frames, rows, cols, width = features.shape
    count = rows * cols
    widened = features.astype(jnp.float32)
    normed = rms_rows(widened).astype(jnp.bfloat16)
    flat = normed.reshape(frames * count, width)
    scale = 1.0 / math.sqrt(width)

    query = project(flat, query_weight).reshape(frames, count, width)
    query_rel = ring_gather(query, "z", halve=True)
    tokens = normed.reshape(frames, count, width)
    half = count // 2
    chains = []
    for part, (first, second) in ((tokens[:, :half], ("y", "x")), (tokens[:, half:], ("x", "y"))):
        inner = jnp.stack(ring_gather(part, first))
        outer = jnp.stack(ring_gather(inner, second, halve=True))
        chains.append(outer.reshape(-1, *outer.shape[2:]))
    query_blocks = jnp.stack(query_rel)
    highest, total, summed, short = attention(query_blocks, chains[0], chains[1], key_weight, value_weight)
    highest, total = highest[:, 0], total[:, 0]

    blocks = len(query_rel)
    first_sent = (blocks // 2, (blocks + 1) // 2 + 1)
    parts = []
    for k in range(blocks):
        lo, hi = k * count, (k + 1) * count
        rows_of = short if k in first_sent else summed
        parts.append((highest[:, lo:hi], total[:, lo:hi], rows_of[:, lo:hi]))
    _, total, summed = ring_reduce(parts, "z", count)
    attended = (summed / total[..., None]).astype(jnp.bfloat16)

    projected = jnp.dot(attended.reshape(-1, width), out_weight, preferred_element_type=jnp.float32)
    mixed = (widened + projected.reshape(features.shape)).astype(jnp.bfloat16)
    mixed_wide = mixed.astype(jnp.float32)
    activated = jax.nn.silu(rms_rows(mixed_wide)).astype(jnp.bfloat16)

    every = ("tm", *ROW_AXES)
    count_rows = 1
    for name in ROW_AXES:
        count_rows *= lax.axis_size(name)
    earlier = lax.ppermute(activated, "tm", [(0, 1)])
    earlier_above = lax.ppermute(activated, every, [(r, count_rows + r + 1) for r in range(count_rows - 1)])
    earlier_below = lax.ppermute(activated, every, [(r + 1, count_rows + r) for r in range(count_rows - 1)])
    above = jnp.concatenate([earlier_above, row_shift(activated, True)], axis=0)
    below = jnp.concatenate([earlier_below, row_shift(activated, False)], axis=0)
    stacked = jnp.concatenate([earlier, activated], axis=0)
    padded = jnp.concatenate([above, stacked, below], axis=1)
    padded = jnp.pad(padded, ((0, 0), (0, 0), (1, 1), (0, 0)))
    patches = []
    for tap_time in range(3):
        for tap_row in range(3):
            for tap_col in range(3):
                patches.append(
                    padded[
                        tap_time : tap_time + frames,
                        tap_row : tap_row + rows,
                        tap_col : tap_col + cols,
                    ]
                )
    columns = jnp.concatenate(patches, axis=-1).reshape(frames * count, 27 * width)
    conv = jnp.dot(
        columns, conv_weight.reshape(27 * width, width), preferred_element_type=jnp.float32
    )
    return (mixed_wide + conv.reshape(features.shape)).astype(jnp.bfloat16)


def solution(mesh):
    sizes = dict(zip(mesh.axis_names, mesh.devices.shape))
    tile = sizes["tile"]
    y = 4
    z = 8
    x = tile // (y * z)
    fine = Mesh(mesh.devices.reshape(sizes["tm"], x, z, y), ("tm", *ROW_AXES))
    spec = P("tm", ROW_AXES, None, None)
    in_specs = (spec, P(), P(), P(), P(), P())
    return jax.shard_map(
        per_device, mesh=fine, in_specs=in_specs, out_specs=spec, check_vma=False
    )
```
